128 devices in a mesh: dp: 4 (over y_hi, core), fsdp: 32 (over x, y_lo, z).
Axes of the slice: x: 4, y: 4 (y_hi: 2, y_lo: 2; y = y_hi * 2 + y_lo), z: 4, core: 2. Of those that a mesh axis runs over, the one named last changes fastest.
Arguments:
- activations: bfloat16 [16384, 8192], P(('dp', 'fsdp')), may hold values from -630 to 630, as said below
- gain: bfloat16 [8192], P('fsdp'), may hold values from 0.25 to 1.75
- key_weight: bfloat16 [8192, 512], P('fsdp'), may hold values from -0.0625 to 0.0625
- key_gain: float32 [128], replicated, may hold values from 0.25 to 1.75
- cotangent: bfloat16 [16384, 512], P(('dp', 'fsdp')), may hold values from -6 to 6
- directions: bfloat16 [8192, 8], P('fsdp'), may hold values from -6 to 6
Outputs:
- ortho_basis: float32 [8192, 8], P('fsdp')
- grad: float32 [8192], P('fsdp')
The draws below stay inside these ranges and needn't reach their ends.
Inputs may be any that keep to these rules, and one draw needn't show every extreme that they name: The block's input activations.
All inputs are finite; a program needn't handle non-finite values.
Results may differ from the reference program's by a relative error of at most 0.01.
Values may be sent and summed in bfloat16 or wider, within the bound.
No kernel may reach another device: no remote copies, remote signals or barrier semaphores. Data moves between devices by JAX's collectives and lax.ppermute only.
A program may use at most 128 MiB of HBM per device.

```python
import math
import jax
import jax.numpy as jnp
from jax import lax

D = 8192
HEADS_KV = 4
HEAD_DIM = 128
DIRS = 8
TOKENS = 16384


def draw_activations(key, part):
    first, second, third = jax.random.split(key, 3)
    row_scale = jnp.exp(jax.random.uniform(second, (TOKENS, 1), minval=0.0, maxval=math.log(10.0)))
    ramp = jnp.exp(math.log(3.0) * jnp.arange(D, dtype=jnp.float32)[None, :] / (D - 1))
    jitter = jnp.exp(jax.random.uniform(third, (1, D), minval=0.0, maxval=math.log(3.5)))
    base = jnp.clip(jax.random.normal(first, (TOKENS, D)), -6.0, 6.0)
    return (base * row_scale * ramp * jitter).astype(jnp.bfloat16)


def block_levels(own_key, shape, cuts, low, high):
    level = 1.0
    for dim, parts in cuts:
        heights = jax.random.uniform(jax.random.fold_in(jax.random.fold_in(own_key, 6), dim), (parts,), jnp.float32, low / len(cuts), high / len(cuts))
        level = level * jnp.repeat(jnp.exp(heights), shape[dim] // parts).reshape((-1,) + (1,) * (len(shape) - 1 - dim))
    return level


def normal_values(own_key, extent, scale, reach, cuts=(), kind=jnp.bfloat16):
    values = jax.random.normal(own_key, extent, jnp.float32) * scale
    if len(cuts) > 0:
        values = block_levels(own_key, extent, cuts, -0.22, 0.18) * values
    return jnp.clip(values, min=-reach, max=reach).astype(kind)


def setup_inputs(seed: int = 0) -> dict:
    splits = jax.random.split(jax.random.key(seed), 7)
    return {
        "activations": draw_activations(jax.random.fold_in(splits[6], 71), 0),
        "gain": jnp.clip(1.0 + 0.15 * jax.random.normal(splits[1], (D,), jnp.float32), 0.25, 1.75).astype(jnp.bfloat16),
        "key_weight": normal_values(splits[2], (D, HEADS_KV * HEAD_DIM), D ** -0.5, 0.0625, ((0, 32),)),
        "key_gain": jnp.clip(1.0 + 0.15 * jax.random.normal(splits[3], (HEAD_DIM,), jnp.float32), 0.25, 1.75),
        "cotangent": normal_values(splits[4], (TOKENS, HEADS_KV * HEAD_DIM), 1.0, 6.0, ((0, 128),)),
        "directions": normal_values(splits[5], (D, DIRS), 1.0, 6.0, ((0, 32),)),
    }


def key_stats(key_rows, weighted_flat):
    shaped = key_rows.reshape(key_rows.shape[0], HEADS_KV, HEAD_DIM)
    key_scale = jnp.sqrt(lax.optimization_barrier(jnp.mean(shaped * shaped, axis=-1, keepdims=True)) + 1e-05)
    unit_keys = shaped / key_scale
    weighted = weighted_flat.reshape(shaped.shape)
    inner_sum = lax.optimization_barrier(jnp.sum(unit_keys * weighted, axis=-1, keepdims=True))
    grad_keys = (weighted - unit_keys * inner_sum / HEAD_DIM) / key_scale
    return (key_scale, unit_keys, weighted, inner_sum, grad_keys)

def second_order(tangent_keys, key_scale, unit_keys, weighted, inner_sum, grad_keys):
    shift_rate = lax.optimization_barrier(jnp.sum(unit_keys * tangent_keys, axis=-1, keepdims=True)) / HEAD_DIM
    unit_change = (tangent_keys - unit_keys * shift_rate) / key_scale
    along = lax.optimization_barrier(jnp.sum(unit_change * weighted, axis=-1, keepdims=True))
    return -(unit_change * inner_sum + unit_keys * along) / (HEAD_DIM * key_scale) - grad_keys * shift_rate / key_scale

def block_terms(input_rows, cot_rows, gain, key_weight, key_gain, directions):
    values = input_rows.astype(jnp.float32)
    normed = values / jnp.sqrt(lax.optimization_barrier(jnp.mean(values * values, axis=1, keepdims=True)) + 1e-05)
    scaled_in = (normed * gain.astype(jnp.float32)[None, :]).astype(jnp.bfloat16)
    key_rows = jnp.dot(scaled_in.astype(jnp.float32), key_weight.astype(jnp.float32), preferred_element_type=jnp.float32)
    weighted_flat = cot_rows.astype(jnp.float32) * jnp.tile(key_gain, HEADS_KV)[None, :]
    key_scale, unit_keys, weighted, inner_sum, grad_keys = key_stats(key_rows, weighted_flat)
    row_count = input_rows.shape[0]
    lifted = (normed[None] * directions.astype(jnp.float32).T[:, None, :]).astype(jnp.bfloat16)
    tangent_keys = jnp.dot(lifted.reshape(-1, D).astype(jnp.float32), key_weight.astype(jnp.float32), preferred_element_type=jnp.float32)
    tangent_keys = tangent_keys.reshape(DIRS, row_count, HEADS_KV, HEAD_DIM)
    second = second_order(tangent_keys, key_scale, unit_keys, weighted, inner_sum, grad_keys)
    back_rows = jnp.concatenate([grad_keys[None], second], axis=0).astype(jnp.bfloat16)
    back_rows = back_rows.reshape(-1, HEADS_KV * HEAD_DIM)
    spread = jnp.dot(back_rows.astype(jnp.float32), key_weight.T.astype(jnp.float32), preferred_element_type=jnp.float32)
    spread = spread.reshape(DIRS + 1, row_count, D)
    return lax.optimization_barrier(jnp.sum(spread * normed[None], axis=1))

def reference(activations, gain, key_weight, key_gain, cotangent, directions):
    token_block = math.gcd(TOKENS, 1024)
    block_count = TOKENS // token_block

    def add_block(running, position):
        begin_row = (position * token_block).astype(jnp.int32)
        input_rows = lax.dynamic_slice_in_dim(activations, begin_row, token_block, 0)
        cot_rows = lax.dynamic_slice_in_dim(cotangent, begin_row, token_block, 0)
        return (running + block_terms(input_rows, cot_rows, gain, key_weight, key_gain, directions), None)
    running, _ = lax.scan(add_block, jnp.zeros((DIRS + 1, D), jnp.float32), jnp.arange(block_count, dtype=jnp.int32))
    terms = running / math.sqrt(TOKENS)
    grad = terms[0]
    images = terms[1:]
    gram_matrix = jnp.dot(images, images.T, precision=lax.Precision.HIGHEST)
    factor = jnp.linalg.cholesky(gram_matrix)
    ortho_basis = math.sqrt(D) * jax.scipy.linalg.solve_triangular(factor, images, lower=True)
    return (ortho_basis.T, grad)
```

```python
import math

import jax
import jax.numpy as jnp
from jax import lax
from jax.experimental import pallas as pl
from jax.experimental.pallas import tpu as pltpu
from jax.sharding import PartitionSpec as P

D = 8192
HEADS_KV = 4
HEAD_DIM = 128
FWD_TILE = 1024
BWD_TILE = 1024


def in_blocks(shard, dim, devices):
    shape = shard.shape
    parts = shard.reshape(*shape[:dim], devices, shape[dim] // devices, *shape[dim + 1 :])
    return jnp.moveaxis(parts, dim, 0)


def sum_at_owner(shard, axis, dim):
    devices = lax.axis_size(axis)
    parts = lax.all_to_all(in_blocks(shard, dim, devices), axis, 0, 0, tiled=True)
    return jnp.sum(parts, axis=0)


def copy_for_each(shard, axis):
    copies = jnp.broadcast_to(shard, (lax.axis_size(axis), *shard.shape))
    return lax.all_to_all(copies, axis, split_axis=0, concat_axis=0, tiled=True)


def of_everyone(shard, axis):
    return copy_for_each(shard, axis).sum(axis=0)


def key_stats(key_rows, weighted_flat):
    shaped = key_rows.reshape(key_rows.shape[0], HEADS_KV, HEAD_DIM)
    key_scale = jnp.sqrt(jnp.mean(shaped * shaped, axis=-1, keepdims=True) + 1e-05)
    unit_keys = shaped / key_scale
    weighted = weighted_flat.reshape(shaped.shape)
    inner_sum = jnp.sum(unit_keys * weighted, axis=-1, keepdims=True)
    grad_keys = (weighted - unit_keys * inner_sum / HEAD_DIM) / key_scale
    return (key_scale, unit_keys, weighted, inner_sum, grad_keys)


def second_order(tangent_keys, key_scale, unit_keys, weighted, inner_sum, grad_keys):
    shift_rate = jnp.sum(unit_keys * tangent_keys, axis=-1, keepdims=True) / HEAD_DIM
    unit_change = (tangent_keys - unit_keys * shift_rate) / key_scale
    along = jnp.sum(unit_change * weighted, axis=-1, keepdims=True)
    return (
        -(unit_change * inner_sum + unit_keys * along) / (HEAD_DIM * key_scale)
        - grad_keys * shift_rate / key_scale
    )


def gather_weight(key_weight, gain, directions):
    rows, width = key_weight.shape
    half = rows // 2
    core = lax.axis_index("dp") % 2
    mine = lax.dynamic_slice_in_dim(key_weight, core * half, half, 0)
    packed = jnp.concatenate([gain[:, None], directions], axis=1).reshape(-1)
    pad_rows = -(-packed.shape[0] // width)
    packed = jnp.pad(packed, (0, pad_rows * width - packed.shape[0])).reshape(pad_rows, width)
    piece = jnp.concatenate([mine, packed], axis=0)
    got = copy_for_each(piece, "fsdp")
    devices = got.shape[0]
    weight_half = got[:, :half, :]
    extras = got[:, half:, :].reshape(devices, -1)[:, : rows * (1 + directions.shape[1])]
    extras = extras.reshape(devices * rows, 1 + directions.shape[1])
    dp = lax.axis_size("dp")
    pairs = [(i, i ^ 1) for i in range(dp)]
    other = lax.ppermute(weight_half, "dp", pairs)
    low = jnp.where(core == 0, weight_half, other)
    high = jnp.where(core == 0, other, weight_half)
    whole = jnp.concatenate([low, high], axis=1).reshape(devices * rows, width)
    return whole, extras


def forward_kernel(act_ref, rms_ref, gd_ref, w_ref, out_ref, lhs_ref):
    k = pl.program_id(0)
    tokens = act_ref.shape[0]
    groups = gd_ref.shape[0]

    @pl.when(k == 0)
    def _():
        out_ref[...] = jnp.zeros_like(out_ref)

    normed = act_ref[...].astype(jnp.float32) / rms_ref[...]
    for j in range(groups):
        lhs_ref[j * tokens : (j + 1) * tokens, :] = (normed * gd_ref[j : j + 1, :]).astype(
            jnp.bfloat16
        )
    out_ref[...] += jnp.dot(lhs_ref[...], w_ref[...], preferred_element_type=jnp.float32)


def forward_rows(activations, rms, gd, whole_weight):
    tokens, width = activations.shape
    groups = gd.shape[0]
    keys = whole_weight.shape[1]
    tile = FWD_TILE
    return pl.pallas_call(
        forward_kernel,
        grid=(width // tile,),
        in_specs=[
            pl.BlockSpec((tokens, tile), lambda k: (0, k)),
            pl.BlockSpec((tokens, 1), lambda k: (0, 0)),
            pl.BlockSpec((groups, tile), lambda k: (0, k)),
            pl.BlockSpec((tile, keys), lambda k: (k, 0)),
        ],
        out_specs=pl.BlockSpec((groups * tokens, keys), lambda k: (0, 0)),
        out_shape=jax.ShapeDtypeStruct((groups * tokens, keys), jnp.float32),
        scratch_shapes=[pltpu.VMEM((groups * tokens, tile), jnp.bfloat16)],
        compiler_params=pltpu.CompilerParams(dimension_semantics=("arbitrary",)),
    )(activations, rms, gd, whole_weight)


def backward_kernel(back_ref, w_ref, act_ref, rms_ref, out_ref):
    tokens = act_ref.shape[0]
    groups = out_ref.shape[0]
    normed = act_ref[...].astype(jnp.float32) / rms_ref[...]
    product = lax.dot_general(
        back_ref[...],
        w_ref[...],
        (((1,), (1,)), ((), ())),
        preferred_element_type=jnp.float32,
    )
    product = product.reshape(groups, tokens, product.shape[1])
    out_ref[...] = jnp.sum(product * normed[None], axis=1)


def backward_terms(back_rows, whole_weight, activations, rms, groups):
    tokens, width = activations.shape
    keys = whole_weight.shape[1]
    tile = BWD_TILE
    return pl.pallas_call(
        backward_kernel,
        grid=(width // tile,),
        in_specs=[
            pl.BlockSpec((groups * tokens, keys), lambda d: (0, 0)),
            pl.BlockSpec((tile, keys), lambda d: (d, 0)),
            pl.BlockSpec((tokens, tile), lambda d: (0, d)),
            pl.BlockSpec((tokens, 1), lambda d: (0, 0)),
        ],
        out_specs=pl.BlockSpec((groups, tile), lambda d: (0, d)),
        out_shape=jax.ShapeDtypeStruct((groups, width), jnp.float32),
        compiler_params=pltpu.CompilerParams(dimension_semantics=("arbitrary",)),
    )(back_rows, whole_weight, activations, rms)


def per_device(activations, gain, key_weight, key_gain, cotangent, directions):
    tokens_dev = activations.shape[0]
    total_tokens = tokens_dev * lax.axis_size("dp") * lax.axis_size("fsdp")
    values = activations.astype(jnp.float32)
    rms = jnp.sqrt(jnp.mean(values * values, axis=1, keepdims=True) + 1e-05)
    width_keys = key_weight.shape[1]
    count_dirs = directions.shape[1]
    groups = count_dirs + 1

    whole_weight, extras = gather_weight(key_weight, gain, directions)
    gd = extras.astype(jnp.float32).T

    forward = forward_rows(activations, rms, gd, whole_weight)
    forward = forward.reshape(groups, tokens_dev, width_keys)
    key_rows = forward[0]
    tangent_flat = forward[1:]
    weighted_flat = cotangent.astype(jnp.float32) * jnp.tile(key_gain, HEADS_KV)[None, :]
    key_scale, unit_keys, weighted, inner_sum, grad_keys = key_stats(key_rows, weighted_flat)
    tangent_keys = tangent_flat.reshape(count_dirs, tokens_dev, HEADS_KV, HEAD_DIM)
    second = second_order(tangent_keys, key_scale, unit_keys, weighted, inner_sum, grad_keys)
    back_rows = jnp.concatenate([grad_keys[None], second], axis=0).astype(jnp.bfloat16)
    back_rows = back_rows.reshape(-1, width_keys)

    partial_terms = backward_terms(back_rows, whole_weight, activations, rms, groups)
    shared_rows = sum_at_owner(partial_terms, "fsdp", 1)
    summed = of_everyone(shared_rows, "dp") / math.sqrt(total_tokens)
    images = summed[1:]
    gram_matrix = of_everyone(
        jnp.dot(images, images.T, precision=lax.Precision.HIGHEST), "fsdp"
    )
    factor = jnp.linalg.cholesky(gram_matrix)
    ortho_basis = math.sqrt(D) * jax.scipy.linalg.solve_triangular(factor, images, lower=True)
    return (ortho_basis.T, summed[0])


def solution(mesh):
    placed = (
        P(("dp", "fsdp"), None),
        P("fsdp"),
        P("fsdp", None),
        P(),
        P(("dp", "fsdp"), None),
        P("fsdp", None),
    )
    return jax.shard_map(
        per_device,
        mesh=mesh,
        in_specs=placed,
        out_specs=(P("fsdp", None), P("fsdp")),
        check_vma=False,
    )
```

```python
import math

import jax
import jax.numpy as jnp
from jax import lax
from jax.experimental import pallas as pl
from jax.experimental.pallas import tpu as pltpu
from jax.sharding import PartitionSpec as P

D = 8192
HEADS_KV = 4
HEAD_DIM = 128
FWD_TILE = 1024
BWD_TILE = 1024


def in_blocks(shard, dim, devices):
    shape = shard.shape
    parts = shard.reshape(*shape[:dim], devices, shape[dim] // devices, *shape[dim + 1 :])
    return jnp.moveaxis(parts, dim, 0)


def sum_at_owner(shard, axis, dim):
    devices = lax.axis_size(axis)
    parts = lax.all_to_all(in_blocks(shard, dim, devices), axis, 0, 0, tiled=True)
    return jnp.sum(parts, axis=0)


def copy_for_each(shard, axis):
    copies = jnp.broadcast_to(shard, (lax.axis_size(axis), *shard.shape))
    return lax.all_to_all(copies, axis, split_axis=0, concat_axis=0, tiled=True)


def of_everyone(shard, axis):
    return copy_for_each(shard, axis).sum(axis=0)


def key_stats(key_rows, weighted_flat):
    shaped = key_rows.reshape(key_rows.shape[0], HEADS_KV, HEAD_DIM)
    key_scale = jnp.sqrt(jnp.mean(shaped * shaped, axis=-1, keepdims=True) + 1e-05)
    unit_keys = shaped / key_scale
    weighted = weighted_flat.reshape(shaped.shape)
    inner_sum = jnp.sum(unit_keys * weighted, axis=-1, keepdims=True)
    grad_keys = (weighted - unit_keys * inner_sum / HEAD_DIM) / key_scale
    return (key_scale, unit_keys, weighted, inner_sum, grad_keys)


def second_order(tangent_keys, key_scale, unit_keys, weighted, inner_sum, grad_keys):
    shift_rate = jnp.sum(unit_keys * tangent_keys, axis=-1, keepdims=True) / HEAD_DIM
    unit_change = (tangent_keys - unit_keys * shift_rate) / key_scale
    along = jnp.sum(unit_change * weighted, axis=-1, keepdims=True)
    return (
        -(unit_change * inner_sum + unit_keys * along) / (HEAD_DIM * key_scale)
        - grad_keys * shift_rate / key_scale
    )


def gather_weight(key_weight, gain, directions):
    rows, width = key_weight.shape
    half = rows // 2
    core = lax.axis_index("dp") % 2
    mine = lax.dynamic_slice_in_dim(key_weight, core * half, half, 0)
    extra = jnp.concatenate([gain[None, :], directions.T], axis=0)
    extra = jnp.pad(extra, ((0, 16 - extra.shape[0]), (0, width - rows)))
    piece = jnp.concatenate([mine, extra], axis=0)
    first = copy_for_each(piece, "fsdp")
    dp = lax.axis_size("dp")
    second = lax.ppermute(first, "dp", [(i, i ^ 1) for i in range(dp)])
    extras = first[:, half : half + 1 + directions.shape[1], :rows]
    extras = jnp.transpose(extras, (1, 0, 2)).reshape(extras.shape[1], -1)
    return first, second, extras.astype(jnp.float32)


def split_halves(values, core):
    lead = values.shape[0]
    blocks = values.reshape(lead, -1, 2, 128)
    low, high = blocks[:, :, 0, :], blocks[:, :, 1, :]
    first = jnp.where(core == 0, low, high).reshape(lead, -1)
    second = jnp.where(core == 0, high, low).reshape(lead, -1)
    return first, second


def join_halves(first, second, core):
    lead = first.shape[0]
    a = first.reshape(lead, -1, 1, 128)
    b = second.reshape(lead, -1, 1, 128)
    low = jnp.where(core == 0, a, b)
    high = jnp.where(core == 0, b, a)
    return jnp.concatenate([low, high], axis=2).reshape(lead, -1)


def middle_rows(acc, cot, key_gain_row, back_ref):
    tokens = cot.shape[0]
    groups = acc.shape[0] // tokens
    weighted_all = cot.astype(jnp.float32) * key_gain_row
    for h in range(HEADS_KV):
        cols = slice(h * HEAD_DIM, (h + 1) * HEAD_DIM)
        key = acc[0:tokens, cols]
        weighted = weighted_all[:, cols]
        key_scale = jnp.sqrt(jnp.sum(key * key, axis=-1, keepdims=True) / HEAD_DIM + 1e-05)
        unit_keys = key / key_scale
        inner_sum = jnp.sum(unit_keys * weighted, axis=-1, keepdims=True)
        grad_keys = (weighted - unit_keys * inner_sum / HEAD_DIM) / key_scale
        back_ref[0:tokens, cols] = grad_keys.astype(back_ref.dtype)
        for j in range(1, groups):
            tangent = acc[j * tokens : (j + 1) * tokens, cols]
            shift_rate = jnp.sum(unit_keys * tangent, axis=-1, keepdims=True) / HEAD_DIM
            unit_change = (tangent - unit_keys * shift_rate) / key_scale
            along = jnp.sum(unit_change * weighted, axis=-1, keepdims=True)
            second = -(unit_change * inner_sum + unit_keys * along) / (
                HEAD_DIM * key_scale
            ) - grad_keys * shift_rate / key_scale
            back_ref[j * tokens : (j + 1) * tokens, cols] = second.astype(back_ref.dtype)


def build_lhs(act_ref, rms_ref, gd_ref, lhs_ref):
    tokens = act_ref.shape[0]
    normed = act_ref[...].astype(jnp.float32) / rms_ref[...]
    for j in range(gd_ref.shape[0]):
        lhs_ref[j * tokens : (j + 1) * tokens, :] = (normed * gd_ref[j : j + 1, :]).astype(
            jnp.bfloat16
        )


def weight_tile(w_ref):
    shards, rows, width = w_ref.shape
    return w_ref[...].reshape(shards * rows, width)


def forward_first_kernel(act_ref, rms_ref, gd_ref, w_ref, out_ref, lhs_ref):
    k = pl.program_id(0)

    @pl.when(k == 0)
    def _():
        out_ref[...] = jnp.zeros_like(out_ref)

    build_lhs(act_ref, rms_ref, gd_ref, lhs_ref)
    out_ref[...] += jnp.dot(lhs_ref[...], weight_tile(w_ref), preferred_element_type=jnp.float32)


def forward_second_kernel(
    act_ref, rms_ref, gd_ref, w_ref, acc_in_ref, cot_ref, kg_ref, back_ref, lhs_ref, acc_ref
):
    k = pl.program_id(0)

    @pl.when(k == 0)
    def _():
        acc_ref[...] = acc_in_ref[...]

    build_lhs(act_ref, rms_ref, gd_ref, lhs_ref)
    acc_ref[...] += jnp.dot(lhs_ref[...], weight_tile(w_ref), preferred_element_type=jnp.float32)

    @pl.when(k == pl.num_programs(0) - 1)
    def _():
        middle_rows(acc_ref[...], cot_ref[...], kg_ref[...], back_ref)


def weight_spec(shards, half, keys):
    return pl.BlockSpec((shards, half, keys), lambda k: (k, 0, 0))


def forward_rows(act_first, act_second, rms, gd_first, gd_second, first, second, cot, kg_row):
    tokens, width = act_first.shape
    groups = gd_first.shape[0]
    keys = first.shape[2]
    half = width // first.shape[0]
    tile = FWD_TILE
    shards = tile // half
    common = [
        pl.BlockSpec((tokens, tile), lambda k: (0, k)),
        pl.BlockSpec((tokens, 1), lambda k: (0, 0)),
        pl.BlockSpec((groups, tile), lambda k: (0, k)),
        weight_spec(shards, half, keys),
    ]
    acc = pl.pallas_call(
        forward_first_kernel,
        grid=(width // tile,),
        in_specs=common,
        out_specs=pl.BlockSpec((groups * tokens, keys), lambda k: (0, 0)),
        out_shape=jax.ShapeDtypeStruct((groups * tokens, keys), jnp.float32),
        scratch_shapes=[pltpu.VMEM((groups * tokens, tile), jnp.bfloat16)],
        compiler_params=pltpu.CompilerParams(dimension_semantics=("arbitrary",)),
    )(act_first, rms, gd_first, first)
    return pl.pallas_call(
        forward_second_kernel,
        grid=(width // tile,),
        in_specs=common
        + [
            pl.BlockSpec((groups * tokens, keys), lambda k: (0, 0)),
            pl.BlockSpec((tokens, keys), lambda k: (0, 0)),
            pl.BlockSpec((1, keys), lambda k: (0, 0)),
        ],
        out_specs=pl.BlockSpec((groups * tokens, keys), lambda k: (0, 0)),
        out_shape=jax.ShapeDtypeStruct((groups * tokens, keys), jnp.bfloat16),
        scratch_shapes=[
            pltpu.VMEM((groups * tokens, tile), jnp.bfloat16),
            pltpu.VMEM((groups * tokens, keys), jnp.float32),
        ],
        compiler_params=pltpu.CompilerParams(dimension_semantics=("arbitrary",)),
    )(act_second, rms, gd_second, second, acc, cot, kg_row)


def backward_kernel(back_ref, w1_ref, w2_ref, act1_ref, act2_ref, rms_ref, out_ref):
    k = pl.program_id(0)
    steps = pl.num_programs(0) // 2
    tokens = act1_ref.shape[0]
    groups = out_ref.shape[0]

    def one(w_ref, act_ref):
        normed = act_ref[...].astype(jnp.float32) / rms_ref[...]
        product = lax.dot_general(
            back_ref[...],
            weight_tile(w_ref),
            (((1,), (1,)), ((), ())),
            preferred_element_type=jnp.float32,
        )
        product = product.reshape(groups, tokens, product.shape[1])
        out_ref[...] = jnp.sum(product * normed[None], axis=1)

    @pl.when(k < steps)
    def _():
        one(w1_ref, act1_ref)

    @pl.when(k >= steps)
    def _():
        one(w2_ref, act2_ref)


def backward_terms(back_rows, first, second, act_first, act_second, rms, groups):
    tokens, width = act_first.shape
    keys = first.shape[2]
    half = width // first.shape[0]
    tile = BWD_TILE
    shards = tile // half
    steps = width // tile
    low = lambda k: jnp.minimum(k, steps - 1)
    high = lambda k: jnp.maximum(k - steps, 0)
    return pl.pallas_call(
        backward_kernel,
        grid=(2 * steps,),
        in_specs=[
            pl.BlockSpec((groups * tokens, keys), lambda k: (0, 0)),
            pl.BlockSpec((shards, half, keys), lambda k: (low(k), 0, 0)),
            pl.BlockSpec((shards, half, keys), lambda k: (high(k), 0, 0)),
            pl.BlockSpec((tokens, tile), lambda k: (0, low(k))),
            pl.BlockSpec((tokens, tile), lambda k: (0, high(k))),
            pl.BlockSpec((tokens, 1), lambda k: (0, 0)),
        ],
        out_specs=pl.BlockSpec((groups, tile), lambda k: (0, k)),
        out_shape=jax.ShapeDtypeStruct((groups, 2 * width), jnp.float32),
        compiler_params=pltpu.CompilerParams(dimension_semantics=("arbitrary",)),
    )(back_rows, first, second, act_first, act_second, rms)


def per_device(activations, gain, key_weight, key_gain, cotangent, directions):
    tokens_dev = activations.shape[0]
    total_tokens = tokens_dev * lax.axis_size("dp") * lax.axis_size("fsdp")
    values = activations.astype(jnp.float32)
    rms = jnp.sqrt(jnp.mean(values * values, axis=1, keepdims=True) + 1e-05)
    width_keys = key_weight.shape[1]
    groups = directions.shape[1] + 1
    core = lax.axis_index("dp") % 2

    first, second, gd = gather_weight(key_weight, gain, directions)
    act_first, act_second = split_halves(activations, core)
    gd_first, gd_second = split_halves(gd, core)
    kg_row = jnp.tile(key_gain, HEADS_KV)[None, :]

    back_rows = forward_rows(
        act_first, act_second, rms, gd_first, gd_second, first, second, cotangent, kg_row
    )
    partial_terms = backward_terms(back_rows, first, second, act_first, act_second, rms, groups)
    half_width = act_first.shape[1]
    partial_terms = join_halves(
        partial_terms[:, :half_width], partial_terms[:, half_width:], core
    )
    shared_rows = sum_at_owner(partial_terms, "fsdp", 1)
    summed = of_everyone(shared_rows, "dp") / math.sqrt(total_tokens)
    images = summed[1:]
    gram_matrix = of_everyone(
        jnp.dot(images, images.T, precision=lax.Precision.HIGHEST), "fsdp"
    )
    factor = jnp.linalg.cholesky(gram_matrix)
    ortho_basis = math.sqrt(D) * jax.scipy.linalg.solve_triangular(factor, images, lower=True)
    return (ortho_basis.T, summed[0])


def solution(mesh):
    placed = (
        P(("dp", "fsdp"), None),
        P("fsdp"),
        P("fsdp", None),
        P(),
        P(("dp", "fsdp"), None),
        P("fsdp", None),
    )
    return jax.shard_map(
        per_device,
        mesh=mesh,
        in_specs=placed,
        out_specs=(P("fsdp", None), P("fsdp")),
        check_vma=False,
    )
```

```python
import math

import jax
import jax.numpy as jnp
from jax import lax
from jax.experimental import pallas as pl
from jax.experimental.pallas import tpu as pltpu
from jax.sharding import PartitionSpec as P

D = 8192
HEADS_KV = 4
HEAD_DIM = 128
HALF = 128
FWD_TILE = 1024
BWD_TILE = 1024


def in_blocks(shard, dim, devices):
    shape = shard.shape
    parts = shard.reshape(*shape[:dim], devices, shape[dim] // devices, *shape[dim + 1 :])
    return jnp.moveaxis(parts, dim, 0)


def sum_at_owner(shard, axis, dim):
    devices = lax.axis_size(axis)
    parts = lax.all_to_all(in_blocks(shard, dim, devices), axis, 0, 0, tiled=True)
    return jnp.sum(parts, axis=0)


def copy_for_each(shard, axis):
    copies = jnp.broadcast_to(shard, (lax.axis_size(axis), *shard.shape))
    return lax.all_to_all(copies, axis, split_axis=0, concat_axis=0, tiled=True)


def of_everyone(shard, axis):
    return copy_for_each(shard, axis).sum(axis=0)


def gather_weight(key_weight, gain, directions):
    rows, width = key_weight.shape
    half = rows // 2
    core = lax.axis_index("dp") % 2
    mine = lax.dynamic_slice_in_dim(key_weight, core * half, half, 0)
    extra = jnp.concatenate([gain[None, :], directions.T], axis=0)
    extra = jnp.pad(extra, ((0, 16 - extra.shape[0]), (0, width - rows)))
    piece = jnp.concatenate([mine, extra], axis=0)
    first = copy_for_each(piece, "fsdp")
    dp = lax.axis_size("dp")
    second = lax.ppermute(first, "dp", [(i, i ^ 1) for i in range(dp)])
    extras = first[:, half : half + 1 + directions.shape[1], :rows]
    extras = jnp.transpose(extras, (1, 0, 2)).reshape(extras.shape[1], -1)
    return first, second, extras.astype(jnp.float32)


def middle_rows(acc, cot, key_gain_row, back_ref):
    tokens = cot.shape[0]
    groups = acc.shape[0] // tokens
    weighted_all = cot.astype(jnp.float32) * key_gain_row
    for h in range(HEADS_KV):
        cols = slice(h * HEAD_DIM, (h + 1) * HEAD_DIM)
        key = acc[0:tokens, cols]
        weighted = weighted_all[:, cols]
        key_scale = jnp.sqrt(jnp.sum(key * key, axis=-1, keepdims=True) / HEAD_DIM + 1e-05)
        unit_keys = key / key_scale
        inner_sum = jnp.sum(unit_keys * weighted, axis=-1, keepdims=True)
        grad_keys = (weighted - unit_keys * inner_sum / HEAD_DIM) / key_scale
        back_ref[0:tokens, cols] = grad_keys.astype(back_ref.dtype)
        for j in range(1, groups):
            tangent = acc[j * tokens : (j + 1) * tokens, cols]
            shift_rate = jnp.sum(unit_keys * tangent, axis=-1, keepdims=True) / HEAD_DIM
            unit_change = (tangent - unit_keys * shift_rate) / key_scale
            along = jnp.sum(unit_change * weighted, axis=-1, keepdims=True)
            second = -(unit_change * inner_sum + unit_keys * along) / (
                HEAD_DIM * key_scale
            ) - grad_keys * shift_rate / key_scale
            back_ref[j * tokens : (j + 1) * tokens, cols] = second.astype(back_ref.dtype)


def build_lhs(act_ref, rms_ref, gd_ref, lhs_ref, offset):
    tokens = act_ref.shape[0]
    shard = 2 * HALF
    for g in range(act_ref.shape[1] // shard):
        cols = slice(g * shard + offset, g * shard + offset + HALF)
        normed = act_ref[:, cols].astype(jnp.float32) / rms_ref[...]
        for j in range(gd_ref.shape[0]):
            lhs_ref[j * tokens : (j + 1) * tokens, g * HALF : (g + 1) * HALF] = (
                normed * gd_ref[j : j + 1, cols]
            ).astype(jnp.bfloat16)


def build_for(core_ref, act_ref, rms_ref, gd_ref, lhs_ref, own):
    for core in range(2):
        offset = (core if own else 1 - core) * HALF

        @pl.when(core_ref[0] == core)
        def _():
            build_lhs(act_ref, rms_ref, gd_ref, lhs_ref, offset)


def weight_tile(w_ref):
    shards, rows, width = w_ref.shape
    return w_ref[...].reshape(shards * rows, width)


def forward_first_kernel(core_ref, act_ref, rms_ref, gd_ref, w_ref, out_ref, lhs_ref):
    k = pl.program_id(0)

    @pl.when(k == 0)
    def _():
        out_ref[...] = jnp.zeros_like(out_ref)

    build_for(core_ref, act_ref, rms_ref, gd_ref, lhs_ref, True)
    out_ref[...] += jnp.dot(lhs_ref[...], weight_tile(w_ref), preferred_element_type=jnp.float32)


def forward_second_kernel(
    core_ref, act_ref, rms_ref, gd_ref, w_ref, acc_in_ref, cot_ref, kg_ref, back_ref, lhs_ref, acc_ref
):
    k = pl.program_id(0)

    @pl.when(k == 0)
    def _():
        acc_ref[...] = acc_in_ref[...]

    build_for(core_ref, act_ref, rms_ref, gd_ref, lhs_ref, False)
    acc_ref[...] += jnp.dot(lhs_ref[...], weight_tile(w_ref), preferred_element_type=jnp.float32)

    @pl.when(k == pl.num_programs(0) - 1)
    def _():
        middle_rows(acc_ref[...], cot_ref[...], kg_ref[...], back_ref)


def forward_rows(core, activations, rms, gd, first, second, cot, kg_row):
    tokens, width = activations.shape
    groups = gd.shape[0]
    keys = first.shape[2]
    tile = 2 * FWD_TILE
    shards = tile // (2 * HALF)
    common = [
        pl.BlockSpec((tokens, tile), lambda k, c: (0, k)),
        pl.BlockSpec((tokens, 1), lambda k, c: (0, 0)),
        pl.BlockSpec((groups, tile), lambda k, c: (0, k)),
        pl.BlockSpec((shards, HALF, keys), lambda k, c: (k, 0, 0)),
    ]
    params = pltpu.CompilerParams(dimension_semantics=("arbitrary",))
    acc = pl.pallas_call(
        forward_first_kernel,
        grid_spec=pltpu.PrefetchScalarGridSpec(
            num_scalar_prefetch=1,
            grid=(width // tile,),
            in_specs=common,
            out_specs=pl.BlockSpec((groups * tokens, keys), lambda k, c: (0, 0)),
            scratch_shapes=[pltpu.VMEM((groups * tokens, FWD_TILE), jnp.bfloat16)],
        ),
        out_shape=jax.ShapeDtypeStruct((groups * tokens, keys), jnp.float32),
        compiler_params=params,
    )(core, activations, rms, gd, first)
    return pl.pallas_call(
        forward_second_kernel,
        grid_spec=pltpu.PrefetchScalarGridSpec(
            num_scalar_prefetch=1,
            grid=(width // tile,),
            in_specs=common
            + [
                pl.BlockSpec((groups * tokens, keys), lambda k, c: (0, 0)),
                pl.BlockSpec((tokens, keys), lambda k, c: (0, 0)),
                pl.BlockSpec((1, keys), lambda k, c: (0, 0)),
            ],
            out_specs=pl.BlockSpec((groups * tokens, keys), lambda k, c: (0, 0)),
            scratch_shapes=[
                pltpu.VMEM((groups * tokens, FWD_TILE), jnp.bfloat16),
                pltpu.VMEM((groups * tokens, keys), jnp.float32),
            ],
        ),
        out_shape=jax.ShapeDtypeStruct((groups * tokens, keys), jnp.bfloat16),
        compiler_params=params,
    )(core, activations, rms, gd, second, acc, cot, kg_row)


def backward_kernel(core_ref, back_ref, w1_ref, w2_ref, act_ref, rms_ref, out_ref):
    tokens = act_ref.shape[0]
    groups = out_ref.shape[0]
    shard = 2 * HALF

    def product_of(w_ref):
        return lax.dot_general(
            back_ref[...],
            weight_tile(w_ref),
            (((1,), (1,)), ((), ())),
            preferred_element_type=jnp.float32,
        )

    own = product_of(w1_ref)
    other = product_of(w2_ref)

    def emit(product, offset):
        for g in range(act_ref.shape[1] // shard):
            cols = slice(g * shard + offset, g * shard + offset + HALF)
            normed = act_ref[:, cols].astype(jnp.float32) / rms_ref[...]
            part = product[:, g * HALF : (g + 1) * HALF].reshape(groups, tokens, HALF)
            out_ref[:, cols] = jnp.sum(part * normed[None], axis=1)

    for core in range(2):

        @pl.when(core_ref[0] == core)
        def _():
            emit(own, core * HALF)
            emit(other, (1 - core) * HALF)


def backward_terms(core, back_rows, first, second, activations, rms, groups):
    tokens, width = activations.shape
    keys = first.shape[2]
    tile = 2 * BWD_TILE
    shards = tile // (2 * HALF)
    return pl.pallas_call(
        backward_kernel,
        grid_spec=pltpu.PrefetchScalarGridSpec(
            num_scalar_prefetch=1,
            grid=(width // tile,),
            in_specs=[
                pl.BlockSpec((groups * tokens, keys), lambda k, c: (0, 0)),
                pl.BlockSpec((shards, HALF, keys), lambda k, c: (k, 0, 0)),
                pl.BlockSpec((shards, HALF, keys), lambda k, c: (k, 0, 0)),
                pl.BlockSpec((tokens, tile), lambda k, c: (0, k)),
                pl.BlockSpec((tokens, 1), lambda k, c: (0, 0)),
            ],
            out_specs=pl.BlockSpec((groups, tile), lambda k, c: (0, k)),
        ),
        out_shape=jax.ShapeDtypeStruct((groups, width), jnp.float32),
        compiler_params=pltpu.CompilerParams(dimension_semantics=("arbitrary",)),
    )(core, back_rows, first, second, activations, rms)


def per_device(activations, gain, key_weight, key_gain, cotangent, directions):
    tokens_dev = activations.shape[0]
    total_tokens = tokens_dev * lax.axis_size("dp") * lax.axis_size("fsdp")
    values = activations.astype(jnp.float32)
    rms = jnp.sqrt(jnp.mean(values * values, axis=1, keepdims=True) + 1e-05)
    groups = directions.shape[1] + 1
    core = (lax.axis_index("dp") % 2).astype(jnp.int32).reshape(1)

    first, second, gd = gather_weight(key_weight, gain, directions)
    kg_row = jnp.tile(key_gain, HEADS_KV)[None, :]

    back_rows = forward_rows(core, activations, rms, gd, first, second, cotangent, kg_row)
    partial_terms = backward_terms(core, back_rows, first, second, activations, rms, groups)
    shared_rows = sum_at_owner(partial_terms, "fsdp", 1)
    summed = of_everyone(shared_rows, "dp") / math.sqrt(total_tokens)
    images = summed[1:]
    gram_matrix = of_everyone(
        jnp.dot(images, images.T, precision=lax.Precision.HIGHEST), "fsdp"
    )
    factor = jnp.linalg.cholesky(gram_matrix)
    ortho_basis = math.sqrt(D) * jax.scipy.linalg.solve_triangular(factor, images, lower=True)
    return (ortho_basis.T, summed[0])


def solution(mesh):
    placed = (
        P(("dp", "fsdp"), None),
        P("fsdp"),
        P("fsdp", None),
        P(),
        P(("dp", "fsdp"), None),
        P("fsdp", None),
    )
    return jax.shard_map(
        per_device,
        mesh=mesh,
        in_specs=placed,
        out_specs=(P("fsdp", None), P("fsdp")),
        check_vma=False,
    )
```

```python
import math

import jax
import jax.numpy as jnp
from jax import lax
from jax.experimental import pallas as pl
from jax.experimental.pallas import tpu as pltpu
from jax.sharding import PartitionSpec as P

D = 8192
HEADS_KV = 4
HEAD_DIM = 128
HALF = 128
FWD_TILE = 1024
BWD_TILE = 1024


def in_blocks(shard, dim, devices):
    shape = shard.shape
    parts = shard.reshape(*shape[:dim], devices, shape[dim] // devices, *shape[dim + 1 :])
    return jnp.moveaxis(parts, dim, 0)


def sum_at_owner(shard, axis, dim):
    devices = lax.axis_size(axis)
    parts = lax.all_to_all(in_blocks(shard, dim, devices), axis, 0, 0, tiled=True)
    return jnp.sum(parts, axis=0)


def copy_for_each(shard, axis):
    copies = jnp.broadcast_to(shard, (lax.axis_size(axis), *shard.shape))
    return lax.all_to_all(copies, axis, split_axis=0, concat_axis=0, tiled=True)


def of_everyone(shard, axis):
    return copy_for_each(shard, axis).sum(axis=0)


def sum_over_pairs(shard, axis):
    devices = lax.axis_size(axis)
    step = 1
    while step < devices:
        shard = shard + lax.ppermute(shard, axis, [(i, i ^ step) for i in range(devices)])
        step *= 2
    return shard


def gather_weight(key_weight, gain, directions):
    rows, width = key_weight.shape
    half = rows // 2
    core = lax.axis_index("dp") % 2
    mine = lax.dynamic_slice_in_dim(key_weight, core * half, half, 0)
    extra = jnp.concatenate([gain[None, :], directions.T], axis=0)
    extra = jnp.pad(extra, ((0, 16 - extra.shape[0]), (0, width - rows)))
    piece = jnp.concatenate([mine, extra], axis=0)
    first = copy_for_each(piece, "fsdp")
    dp = lax.axis_size("dp")
    second = lax.ppermute(first, "dp", [(i, i ^ 1) for i in range(dp)])
    extras = first[:, half : half + 1 + directions.shape[1], :rows]
    extras = jnp.transpose(extras, (1, 0, 2)).reshape(extras.shape[1], -1)
    return first, second, extras.astype(jnp.float32)


def middle_rows(acc, cot, key_gain_row, back_ref):
    tokens = cot.shape[0]
    groups = acc.shape[0] // tokens
    weighted_all = cot.astype(jnp.float32) * key_gain_row
    for h in range(HEADS_KV):
        cols = slice(h * HEAD_DIM, (h + 1) * HEAD_DIM)
        key = acc[0:tokens, cols]
        weighted = weighted_all[:, cols]
        key_scale = jnp.sqrt(jnp.sum(key * key, axis=-1, keepdims=True) / HEAD_DIM + 1e-05)
        unit_keys = key / key_scale
        inner_sum = jnp.sum(unit_keys * weighted, axis=-1, keepdims=True)
        grad_keys = (weighted - unit_keys * inner_sum / HEAD_DIM) / key_scale
        back_ref[0:tokens, cols] = grad_keys.astype(back_ref.dtype)
        for j in range(1, groups):
            tangent = acc[j * tokens : (j + 1) * tokens, cols]
            shift_rate = jnp.sum(unit_keys * tangent, axis=-1, keepdims=True) / HEAD_DIM
            unit_change = (tangent - unit_keys * shift_rate) / key_scale
            along = jnp.sum(unit_change * weighted, axis=-1, keepdims=True)
            second = -(unit_change * inner_sum + unit_keys * along) / (
                HEAD_DIM * key_scale
            ) - grad_keys * shift_rate / key_scale
            back_ref[j * tokens : (j + 1) * tokens, cols] = second.astype(back_ref.dtype)


def build_lhs(act_ref, rms_ref, gd_ref, lhs_ref, offset):
    tokens = act_ref.shape[0]
    shard = 2 * HALF
    for g in range(act_ref.shape[1] // shard):
        cols = slice(g * shard + offset, g * shard + offset + HALF)
        normed = act_ref[:, cols].astype(jnp.float32) / rms_ref[...]
        for j in range(gd_ref.shape[0]):
            lhs_ref[j * tokens : (j + 1) * tokens, g * HALF : (g + 1) * HALF] = (
                normed * gd_ref[j : j + 1, cols]
            ).astype(jnp.bfloat16)


def build_for(core_ref, act_ref, rms_ref, gd_ref, lhs_ref, own):
    for core in range(2):
        offset = (core if own else 1 - core) * HALF

        @pl.when(core_ref[0] == core)
        def _():
            build_lhs(act_ref, rms_ref, gd_ref, lhs_ref, offset)


def weight_tile(w_ref):
    shards, rows, width = w_ref.shape
    return w_ref[...].reshape(shards * rows, width)


def forward_first_kernel(core_ref, act_ref, rms_ref, gd_ref, w_ref, out_ref, lhs_ref):
    k = pl.program_id(0)

    @pl.when(k == 0)
    def _():
        out_ref[...] = jnp.zeros_like(out_ref)

    build_for(core_ref, act_ref, rms_ref, gd_ref, lhs_ref, True)
    out_ref[...] += jnp.dot(lhs_ref[...], weight_tile(w_ref), preferred_element_type=jnp.float32)


def forward_second_kernel(
    core_ref, act_ref, rms_ref, gd_ref, w_ref, acc_in_ref, cot_ref, kg_ref, back_ref, lhs_ref, acc_ref
):
    k = pl.program_id(0)

    @pl.when(k == 0)
    def _():
        acc_ref[...] = acc_in_ref[...]

    build_for(core_ref, act_ref, rms_ref, gd_ref, lhs_ref, False)
    acc_ref[...] += jnp.dot(lhs_ref[...], weight_tile(w_ref), preferred_element_type=jnp.float32)

    @pl.when(k == pl.num_programs(0) - 1)
    def _():
        middle_rows(acc_ref[...], cot_ref[...], kg_ref[...], back_ref)


def forward_rows(core, activations, rms, gd, first, second, cot, kg_row):
    tokens, width = activations.shape
    groups = gd.shape[0]
    keys = first.shape[2]
    tile = 2 * FWD_TILE
    shards = tile // (2 * HALF)
    common = [
        pl.BlockSpec((tokens, tile), lambda k, c: (0, k)),
        pl.BlockSpec((tokens, 1), lambda k, c: (0, 0)),
        pl.BlockSpec((groups, tile), lambda k, c: (0, k)),
        pl.BlockSpec((shards, HALF, keys), lambda k, c: (k, 0, 0)),
    ]
    params = pltpu.CompilerParams(dimension_semantics=("arbitrary",))
    acc = pl.pallas_call(
        forward_first_kernel,
        grid_spec=pltpu.PrefetchScalarGridSpec(
            num_scalar_prefetch=1,
            grid=(width // tile,),
            in_specs=common,
            out_specs=pl.BlockSpec((groups * tokens, keys), lambda k, c: (0, 0)),
            scratch_shapes=[pltpu.VMEM((groups * tokens, FWD_TILE), jnp.bfloat16)],
        ),
        out_shape=jax.ShapeDtypeStruct((groups * tokens, keys), jnp.float32),
        compiler_params=params,
    )(core, activations, rms, gd, first)
    return pl.pallas_call(
        forward_second_kernel,
        grid_spec=pltpu.PrefetchScalarGridSpec(
            num_scalar_prefetch=1,
            grid=(width // tile,),
            in_specs=common
            + [
                pl.BlockSpec((groups * tokens, keys), lambda k, c: (0, 0)),
                pl.BlockSpec((tokens, keys), lambda k, c: (0, 0)),
                pl.BlockSpec((1, keys), lambda k, c: (0, 0)),
            ],
            out_specs=pl.BlockSpec((groups * tokens, keys), lambda k, c: (0, 0)),
            scratch_shapes=[
                pltpu.VMEM((groups * tokens, FWD_TILE), jnp.bfloat16),
                pltpu.VMEM((groups * tokens, keys), jnp.float32),
            ],
        ),
        out_shape=jax.ShapeDtypeStruct((groups * tokens, keys), jnp.bfloat16),
        compiler_params=params,
    )(core, activations, rms, gd, second, acc, cot, kg_row)


def backward_kernel(core_ref, back_ref, w1_ref, w2_ref, act_ref, rms_ref, out_ref):
    tokens = act_ref.shape[0]
    groups = out_ref.shape[0]
    shard = 2 * HALF

    def product_of(w_ref):
        return lax.dot_general(
            back_ref[...],
            weight_tile(w_ref),
            (((1,), (1,)), ((), ())),
            preferred_element_type=jnp.float32,
        )

    own = product_of(w1_ref)
    other = product_of(w2_ref)

    def emit(product, offset):
        for g in range(act_ref.shape[1] // shard):
            cols = slice(g * shard + offset, g * shard + offset + HALF)
            normed = act_ref[:, cols].astype(jnp.float32) / rms_ref[...]
            part = product[:, g * HALF : (g + 1) * HALF].reshape(groups, tokens, HALF)
            out_ref[:, cols] = jnp.sum(part * normed[None], axis=1)

    for core in range(2):

        @pl.when(core_ref[0] == core)
        def _():
            emit(own, core * HALF)
            emit(other, (1 - core) * HALF)


def backward_terms(core, back_rows, first, second, activations, rms, groups):
    tokens, width = activations.shape
    keys = first.shape[2]
    tile = 2 * BWD_TILE
    shards = tile // (2 * HALF)
    return pl.pallas_call(
        backward_kernel,
        grid_spec=pltpu.PrefetchScalarGridSpec(
            num_scalar_prefetch=1,
            grid=(width // tile,),
            in_specs=[
                pl.BlockSpec((groups * tokens, keys), lambda k, c: (0, 0)),
                pl.BlockSpec((shards, HALF, keys), lambda k, c: (k, 0, 0)),
                pl.BlockSpec((shards, HALF, keys), lambda k, c: (k, 0, 0)),
                pl.BlockSpec((tokens, tile), lambda k, c: (0, k)),
                pl.BlockSpec((tokens, 1), lambda k, c: (0, 0)),
            ],
            out_specs=pl.BlockSpec((groups, tile), lambda k, c: (0, k)),
        ),
        out_shape=jax.ShapeDtypeStruct((groups, width), jnp.float32),
        compiler_params=pltpu.CompilerParams(dimension_semantics=("arbitrary",)),
    )(core, back_rows, first, second, activations, rms)


def per_device(activations, gain, key_weight, key_gain, cotangent, directions):
    tokens_dev = activations.shape[0]
    total_tokens = tokens_dev * lax.axis_size("dp") * lax.axis_size("fsdp")
    values = activations.astype(jnp.float32)
    rms = jnp.sqrt(jnp.mean(values * values, axis=1, keepdims=True) + 1e-05)
    groups = directions.shape[1] + 1
    core = (lax.axis_index("dp") % 2).astype(jnp.int32).reshape(1)

    first, second, gd = gather_weight(key_weight, gain, directions)
    kg_row = jnp.tile(key_gain, HEADS_KV)[None, :]

    back_rows = forward_rows(core, activations, rms, gd, first, second, cotangent, kg_row)
    partial_terms = backward_terms(core, back_rows, first, second, activations, rms, groups)
    shared_rows = sum_at_owner(partial_terms, "fsdp", 1)
    summed = sum_over_pairs(shared_rows, "dp") / math.sqrt(total_tokens)
    images = summed[1:]
    gram_matrix = of_everyone(
        jnp.dot(images, images.T, precision=lax.Precision.HIGHEST), "fsdp"
    )
    factor = jnp.linalg.cholesky(gram_matrix)
    ortho_basis = math.sqrt(D) * jax.scipy.linalg.solve_triangular(factor, images, lower=True)
    return (ortho_basis.T, summed[0])


def solution(mesh):
    placed = (
        P(("dp", "fsdp"), None),
        P("fsdp"),
        P("fsdp", None),
        P(),
        P(("dp", "fsdp"), None),
        P("fsdp", None),
    )
    return jax.shard_map(
        per_device,
        mesh=mesh,
        in_specs=placed,
        out_specs=(P("fsdp", None), P("fsdp")),
        check_vma=False,
    )
```

```python
import math

import jax
import jax.numpy as jnp
from jax import lax
from jax.experimental import pallas as pl
from jax.experimental.pallas import tpu as pltpu
from jax.sharding import PartitionSpec as P

D = 8192
HEADS_KV = 4
HEAD_DIM = 128
HALF = 128
FWD_TILE = 1024
BWD_TILE = 1024


def in_blocks(shard, dim, devices):
    shape = shard.shape
    parts = shard.reshape(*shape[:dim], devices, shape[dim] // devices, *shape[dim + 1 :])
    return jnp.moveaxis(parts, dim, 0)


def sum_at_owner(shard, axis, dim):
    devices = lax.axis_size(axis)
    parts = lax.all_to_all(in_blocks(shard, dim, devices), axis, 0, 0, tiled=True)
    return jnp.sum(parts, axis=0)


def copy_for_each(shard, axis):
    copies = jnp.broadcast_to(shard, (lax.axis_size(axis), *shard.shape))
    return lax.all_to_all(copies, axis, split_axis=0, concat_axis=0, tiled=True)


def of_everyone(shard, axis):
    return copy_for_each(shard, axis).sum(axis=0)


def sum_over_pairs(shard, axis):
    devices = lax.axis_size(axis)
    step = 1
    while step < devices:
        shard = shard + lax.ppermute(shard, axis, [(i, i ^ step) for i in range(devices)])
        step *= 2
    return shard


def gather_weight(key_weight, gain, directions):
    rows, width = key_weight.shape
    half = rows // 2
    core = lax.axis_index("dp") % 2
    mine = lax.dynamic_slice_in_dim(key_weight, core * half, half, 0)
    extra = jnp.concatenate([gain[None, :], directions.T], axis=0)
    extra = jnp.pad(extra, ((0, 16 - extra.shape[0]), (0, width - rows)))
    piece = jnp.concatenate([mine, extra], axis=0)
    first = copy_for_each(piece, "fsdp")
    dp = lax.axis_size("dp")
    second = lax.ppermute(first, "dp", [(i, i ^ 1) for i in range(dp)])
    extras = first[:, half : half + 1 + directions.shape[1], :rows]
    extras = jnp.transpose(extras, (1, 0, 2)).reshape(extras.shape[1], -1)
    return first, second, extras.astype(jnp.float32)


def middle_rows(acc, cot, key_gain_row, back_ref):
    tokens = cot.shape[0]
    groups = acc.shape[0] // tokens
    weighted_all = cot.astype(jnp.float32) * key_gain_row
    for h in range(HEADS_KV):
        cols = slice(h * HEAD_DIM, (h + 1) * HEAD_DIM)
        key = acc[0:tokens, cols]
        weighted = weighted_all[:, cols]
        key_scale = jnp.sqrt(jnp.sum(key * key, axis=-1, keepdims=True) / HEAD_DIM + 1e-05)
        unit_keys = key / key_scale
        inner_sum = jnp.sum(unit_keys * weighted, axis=-1, keepdims=True)
        grad_keys = (weighted - unit_keys * inner_sum / HEAD_DIM) / key_scale
        back_ref[0:tokens, cols] = grad_keys.astype(back_ref.dtype)
        for j in range(1, groups):
            tangent = acc[j * tokens : (j + 1) * tokens, cols]
            shift_rate = jnp.sum(unit_keys * tangent, axis=-1, keepdims=True) / HEAD_DIM
            unit_change = (tangent - unit_keys * shift_rate) / key_scale
            along = jnp.sum(unit_change * weighted, axis=-1, keepdims=True)
            second = -(unit_change * inner_sum + unit_keys * along) / (
                HEAD_DIM * key_scale
            ) - grad_keys * shift_rate / key_scale
            back_ref[j * tokens : (j + 1) * tokens, cols] = second.astype(back_ref.dtype)


def build_lhs(act_ref, rms_ref, gd_ref, lhs_ref, offset):
    tokens = act_ref.shape[0]
    shard = 2 * HALF
    for g in range(act_ref.shape[1] // shard):
        cols = pl.ds(pl.multiple_of(g * shard + offset, HALF), HALF)
        normed = act_ref[:, cols].astype(jnp.float32) / rms_ref[...]
        gd = gd_ref[:, cols]
        for j in range(gd_ref.shape[0]):
            lhs_ref[j * tokens : (j + 1) * tokens, g * HALF : (g + 1) * HALF] = (
                normed * gd[j : j + 1, :]
            ).astype(jnp.bfloat16)


def build_for(core_ref, act_ref, rms_ref, gd_ref, lhs_ref, own):
    core = core_ref[0] if own else 1 - core_ref[0]
    build_lhs(act_ref, rms_ref, gd_ref, lhs_ref, core * HALF)


def weight_tile(w_ref):
    shards, rows, width = w_ref.shape
    return w_ref[...].reshape(shards * rows, width)


def forward_first_kernel(core_ref, act_ref, rms_ref, gd_ref, w_ref, out_ref, lhs_ref):
    k = pl.program_id(0)

    @pl.when(k == 0)
    def _():
        out_ref[...] = jnp.zeros_like(out_ref)

    build_for(core_ref, act_ref, rms_ref, gd_ref, lhs_ref, True)
    out_ref[...] += jnp.dot(lhs_ref[...], weight_tile(w_ref), preferred_element_type=jnp.float32)


def forward_second_kernel(
    core_ref, act_ref, rms_ref, gd_ref, w_ref, acc_in_ref, cot_ref, kg_ref, back_ref, lhs_ref, acc_ref
):
    k = pl.program_id(0)

    @pl.when(k == 0)
    def _():
        acc_ref[...] = acc_in_ref[...]

    build_for(core_ref, act_ref, rms_ref, gd_ref, lhs_ref, False)
    acc_ref[...] += jnp.dot(lhs_ref[...], weight_tile(w_ref), preferred_element_type=jnp.float32)

    @pl.when(k == pl.num_programs(0) - 1)
    def _():
        middle_rows(acc_ref[...], cot_ref[...], kg_ref[...], back_ref)


def forward_rows(core, activations, rms, gd, first, second, cot, kg_row):
    tokens, width = activations.shape
    groups = gd.shape[0]
    keys = first.shape[2]
    tile = 2 * FWD_TILE
    shards = tile // (2 * HALF)
    common = [
        pl.BlockSpec((tokens, tile), lambda k, c: (0, k)),
        pl.BlockSpec((tokens, 1), lambda k, c: (0, 0)),
        pl.BlockSpec((groups, tile), lambda k, c: (0, k)),
        pl.BlockSpec((shards, HALF, keys), lambda k, c: (k, 0, 0)),
    ]
    params = pltpu.CompilerParams(dimension_semantics=("arbitrary",))
    acc = pl.pallas_call(
        forward_first_kernel,
        grid_spec=pltpu.PrefetchScalarGridSpec(
            num_scalar_prefetch=1,
            grid=(width // tile,),
            in_specs=common,
            out_specs=pl.BlockSpec((groups * tokens, keys), lambda k, c: (0, 0)),
            scratch_shapes=[pltpu.VMEM((groups * tokens, FWD_TILE), jnp.bfloat16)],
        ),
        out_shape=jax.ShapeDtypeStruct((groups * tokens, keys), jnp.float32),
        compiler_params=params,
    )(core, activations, rms, gd, first)
    return pl.pallas_call(
        forward_second_kernel,
        grid_spec=pltpu.PrefetchScalarGridSpec(
            num_scalar_prefetch=1,
            grid=(width // tile,),
            in_specs=common
            + [
                pl.BlockSpec((groups * tokens, keys), lambda k, c: (0, 0)),
                pl.BlockSpec((tokens, keys), lambda k, c: (0, 0)),
                pl.BlockSpec((1, keys), lambda k, c: (0, 0)),
            ],
            out_specs=pl.BlockSpec((groups * tokens, keys), lambda k, c: (0, 0)),
            scratch_shapes=[
                pltpu.VMEM((groups * tokens, FWD_TILE), jnp.bfloat16),
                pltpu.VMEM((groups * tokens, keys), jnp.float32),
            ],
        ),
        out_shape=jax.ShapeDtypeStruct((groups * tokens, keys), jnp.bfloat16),
        compiler_params=params,
    )(core, activations, rms, gd, second, acc, cot, kg_row)


def backward_kernel(core_ref, back_ref, w1_ref, w2_ref, act_ref, rms_ref, out_ref):
    tokens = act_ref.shape[0]
    groups = out_ref.shape[0]
    shard = 2 * HALF

    def product_of(w_ref):
        return lax.dot_general(
            back_ref[...],
            weight_tile(w_ref),
            (((1,), (1,)), ((), ())),
            preferred_element_type=jnp.float32,
        )

    own = product_of(w1_ref)
    other = product_of(w2_ref)

    def emit(product, offset):
        for g in range(act_ref.shape[1] // shard):
            cols = pl.ds(pl.multiple_of(g * shard + offset, HALF), HALF)
            normed = act_ref[:, cols].astype(jnp.float32) / rms_ref[...]
            part = product[:, g * HALF : (g + 1) * HALF].reshape(groups, tokens, HALF)
            out_ref[:, cols] = jnp.sum(part * normed[None], axis=1)

    core = core_ref[0]
    emit(own, core * HALF)
    emit(other, (1 - core) * HALF)


def backward_terms(core, back_rows, first, second, activations, rms, groups):
    tokens, width = activations.shape
    keys = first.shape[2]
    tile = 2 * BWD_TILE
    shards = tile // (2 * HALF)
    return pl.pallas_call(
        backward_kernel,
        grid_spec=pltpu.PrefetchScalarGridSpec(
            num_scalar_prefetch=1,
            grid=(width // tile,),
            in_specs=[
                pl.BlockSpec((groups * tokens, keys), lambda k, c: (0, 0)),
                pl.BlockSpec((shards, HALF, keys), lambda k, c: (k, 0, 0)),
                pl.BlockSpec((shards, HALF, keys), lambda k, c: (k, 0, 0)),
                pl.BlockSpec((tokens, tile), lambda k, c: (0, k)),
                pl.BlockSpec((tokens, 1), lambda k, c: (0, 0)),
            ],
            out_specs=pl.BlockSpec((groups, tile), lambda k, c: (0, k)),
        ),
        out_shape=jax.ShapeDtypeStruct((groups, width), jnp.float32),
        compiler_params=pltpu.CompilerParams(dimension_semantics=("arbitrary",)),
    )(core, back_rows, first, second, activations, rms)


def per_device(activations, gain, key_weight, key_gain, cotangent, directions):
    tokens_dev = activations.shape[0]
    total_tokens = tokens_dev * lax.axis_size("dp") * lax.axis_size("fsdp")
    values = activations.astype(jnp.float32)
    rms = jnp.sqrt(jnp.mean(values * values, axis=1, keepdims=True) + 1e-05)
    groups = directions.shape[1] + 1
    core = (lax.axis_index("dp") % 2).astype(jnp.int32).reshape(1)

    first, second, gd = gather_weight(key_weight, gain, directions)
    kg_row = jnp.tile(key_gain, HEADS_KV)[None, :]

    back_rows = forward_rows(core, activations, rms, gd, first, second, cotangent, kg_row)
    partial_terms = backward_terms(core, back_rows, first, second, activations, rms, groups)
    shared_rows = sum_at_owner(partial_terms, "fsdp", 1)
    summed = sum_over_pairs(shared_rows, "dp") / math.sqrt(total_tokens)
    images = summed[1:]
    gram_matrix = of_everyone(
        jnp.dot(images, images.T, precision=lax.Precision.HIGHEST), "fsdp"
    )
    factor = jnp.linalg.cholesky(gram_matrix)
    ortho_basis = math.sqrt(D) * jax.scipy.linalg.solve_triangular(factor, images, lower=True)
    return (ortho_basis.T, summed[0])


def solution(mesh):
    placed = (
        P(("dp", "fsdp"), None),
        P("fsdp"),
        P("fsdp", None),
        P(),
        P(("dp", "fsdp"), None),
        P("fsdp", None),
    )
    return jax.shard_map(
        per_device,
        mesh=mesh,
        in_specs=placed,
        out_specs=(P("fsdp", None), P("fsdp")),
        check_vma=False,
    )
```

```python
import math

import jax
import jax.numpy as jnp
from jax import lax
from jax.experimental import pallas as pl
from jax.experimental.pallas import tpu as pltpu
from jax.sharding import PartitionSpec as P

D = 8192
HEADS_KV = 4
HEAD_DIM = 128
HALF = 128
FWD_TILE = 1024
BWD_TILE = 1024


def in_blocks(shard, dim, devices):
    shape = shard.shape
    parts = shard.reshape(*shape[:dim], devices, shape[dim] // devices, *shape[dim + 1 :])
    return jnp.moveaxis(parts, dim, 0)


def sum_at_owner(shard, axis, dim):
    devices = lax.axis_size(axis)
    parts = lax.all_to_all(in_blocks(shard, dim, devices), axis, 0, 0, tiled=True)
    return jnp.sum(parts, axis=0)


def copy_for_each(shard, axis):
    copies = jnp.broadcast_to(shard, (lax.axis_size(axis), *shard.shape))
    return lax.all_to_all(copies, axis, split_axis=0, concat_axis=0, tiled=True)


def of_everyone(shard, axis):
    return copy_for_each(shard, axis).sum(axis=0)


def sum_over_pairs(shard, axis):
    devices = lax.axis_size(axis)
    step = 1
    while step < devices:
        shard = shard + lax.ppermute(shard, axis, [(i, i ^ step) for i in range(devices)])
        step *= 2
    return shard


def gather_weight(key_weight, gain, directions):
    rows, width = key_weight.shape
    half = rows // 2
    core = lax.axis_index("dp") % 2
    mine = lax.dynamic_slice_in_dim(key_weight, core * half, half, 0)
    extra = jnp.concatenate([gain[None, :], directions.T], axis=0)
    extra = jnp.pad(extra, ((0, 16 - extra.shape[0]), (0, width - rows)))
    piece = jnp.concatenate([mine, extra], axis=0)
    first = copy_for_each(piece, "fsdp")
    dp = lax.axis_size("dp")
    second = lax.ppermute(first, "dp", [(i, i ^ 1) for i in range(dp)])
    extras = first[:, half : half + 1 + directions.shape[1], :rows]
    extras = jnp.transpose(extras, (1, 0, 2)).reshape(extras.shape[1], -1)
    return first, second, extras.astype(jnp.float32)


def middle_rows(acc, cot, key_gain_row, back_ref):
    tokens = cot.shape[0]
    groups = acc.shape[0] // tokens
    weighted_all = cot.astype(jnp.float32) * key_gain_row
    for h in range(HEADS_KV):
        cols = slice(h * HEAD_DIM, (h + 1) * HEAD_DIM)
        key = acc[0:tokens, cols]
        weighted = weighted_all[:, cols]
        key_scale = jnp.sqrt(jnp.sum(key * key, axis=-1, keepdims=True) / HEAD_DIM + 1e-05)
        inv_scale = 1.0 / key_scale
        unit_keys = key * inv_scale
        inner_sum = jnp.sum(unit_keys * weighted, axis=-1, keepdims=True)
        grad_keys = (weighted - unit_keys * inner_sum / HEAD_DIM) * inv_scale
        back_ref[0:tokens, cols] = grad_keys.astype(back_ref.dtype)
        inv_outer = 1.0 / (HEAD_DIM * key_scale)
        for j in range(1, groups):
            tangent = acc[j * tokens : (j + 1) * tokens, cols]
            shift_rate = jnp.sum(unit_keys * tangent, axis=-1, keepdims=True) / HEAD_DIM
            unit_change = (tangent - unit_keys * shift_rate) * inv_scale
            along = jnp.sum(unit_change * weighted, axis=-1, keepdims=True)
            second = -(unit_change * inner_sum + unit_keys * along) * inv_outer - grad_keys * (
                shift_rate * inv_scale
            )
            back_ref[j * tokens : (j + 1) * tokens, cols] = second.astype(back_ref.dtype)


def build_lhs(act_ref, inv_rms_ref, gd_ref, lhs_ref, offset):
    tokens = act_ref.shape[0]
    shard = 2 * HALF
    for g in range(act_ref.shape[1] // shard):
        cols = pl.ds(pl.multiple_of(g * shard + offset, HALF), HALF)
        normed = act_ref[:, cols].astype(jnp.float32) * inv_rms_ref[...]
        gd = gd_ref[:, cols]
        for j in range(gd_ref.shape[0]):
            lhs_ref[j * tokens : (j + 1) * tokens, g * HALF : (g + 1) * HALF] = (
                normed * gd[j : j + 1, :]
            ).astype(jnp.bfloat16)


def build_for(core_ref, act_ref, inv_rms_ref, gd_ref, lhs_ref, own):
    core = core_ref[0] if own else 1 - core_ref[0]
    build_lhs(act_ref, inv_rms_ref, gd_ref, lhs_ref, core * HALF)


def weight_tile(w_ref):
    shards, rows, width = w_ref.shape
    return w_ref[...].reshape(shards * rows, width)


def forward_first_kernel(core_ref, act_ref, inv_rms_ref, gd_ref, w_ref, out_ref, lhs_ref):
    k = pl.program_id(0)

    @pl.when(k == 0)
    def _():
        out_ref[...] = jnp.zeros_like(out_ref)

    build_for(core_ref, act_ref, inv_rms_ref, gd_ref, lhs_ref, True)
    out_ref[...] += jnp.dot(lhs_ref[...], weight_tile(w_ref), preferred_element_type=jnp.float32)


def forward_second_kernel(
    core_ref, act_ref, inv_rms_ref, gd_ref, w_ref, acc_in_ref, cot_ref, kg_ref, back_ref, lhs_ref, acc_ref
):
    k = pl.program_id(0)

    @pl.when(k == 0)
    def _():
        acc_ref[...] = acc_in_ref[...]

    build_for(core_ref, act_ref, inv_rms_ref, gd_ref, lhs_ref, False)
    acc_ref[...] += jnp.dot(lhs_ref[...], weight_tile(w_ref), preferred_element_type=jnp.float32)

    @pl.when(k == pl.num_programs(0) - 1)
    def _():
        middle_rows(acc_ref[...], cot_ref[...], kg_ref[...], back_ref)


def forward_rows(core, activations, inv_rms, gd, first, second, cot, kg_row):
    tokens, width = activations.shape
    groups = gd.shape[0]
    keys = first.shape[2]
    tile = 2 * FWD_TILE
    shards = tile // (2 * HALF)
    common = [
        pl.BlockSpec((tokens, tile), lambda k, c: (0, k)),
        pl.BlockSpec((tokens, 1), lambda k, c: (0, 0)),
        pl.BlockSpec((groups, tile), lambda k, c: (0, k)),
        pl.BlockSpec((shards, HALF, keys), lambda k, c: (k, 0, 0)),
    ]
    params = pltpu.CompilerParams(dimension_semantics=("arbitrary",))
    acc = pl.pallas_call(
        forward_first_kernel,
        grid_spec=pltpu.PrefetchScalarGridSpec(
            num_scalar_prefetch=1,
            grid=(width // tile,),
            in_specs=common,
            out_specs=pl.BlockSpec((groups * tokens, keys), lambda k, c: (0, 0)),
            scratch_shapes=[pltpu.VMEM((groups * tokens, FWD_TILE), jnp.bfloat16)],
        ),
        out_shape=jax.ShapeDtypeStruct((groups * tokens, keys), jnp.float32),
        compiler_params=params,
    )(core, activations, inv_rms, gd, first)
    return pl.pallas_call(
        forward_second_kernel,
        grid_spec=pltpu.PrefetchScalarGridSpec(
            num_scalar_prefetch=1,
            grid=(width // tile,),
            in_specs=common
            + [
                pl.BlockSpec((groups * tokens, keys), lambda k, c: (0, 0)),
                pl.BlockSpec((tokens, keys), lambda k, c: (0, 0)),
                pl.BlockSpec((1, keys), lambda k, c: (0, 0)),
            ],
            out_specs=pl.BlockSpec((groups * tokens, keys), lambda k, c: (0, 0)),
            scratch_shapes=[
                pltpu.VMEM((groups * tokens, FWD_TILE), jnp.bfloat16),
                pltpu.VMEM((groups * tokens, keys), jnp.float32),
            ],
        ),
        out_shape=jax.ShapeDtypeStruct((groups * tokens, keys), jnp.bfloat16),
        compiler_params=params,
    )(core, activations, inv_rms, gd, second, acc, cot, kg_row)


def backward_kernel(core_ref, back_ref, w1_ref, w2_ref, act_ref, inv_rms_ref, out_ref):
    tokens = act_ref.shape[0]
    groups = out_ref.shape[0]
    shard = 2 * HALF

    def product_of(w_ref):
        return lax.dot_general(
            back_ref[...],
            weight_tile(w_ref),
            (((1,), (1,)), ((), ())),
            preferred_element_type=jnp.float32,
        )

    own = product_of(w1_ref)
    other = product_of(w2_ref)

    def emit(product, offset):
        for g in range(act_ref.shape[1] // shard):
            cols = pl.ds(pl.multiple_of(g * shard + offset, HALF), HALF)
            normed = act_ref[:, cols].astype(jnp.float32) * inv_rms_ref[...]
            part = product[:, g * HALF : (g + 1) * HALF].reshape(groups, tokens, HALF)
            out_ref[:, cols] = jnp.sum(part * normed[None], axis=1)

    core = core_ref[0]
    emit(own, core * HALF)
    emit(other, (1 - core) * HALF)


def backward_terms(core, back_rows, first, second, activations, inv_rms, groups):
    tokens, width = activations.shape
    keys = first.shape[2]
    tile = 2 * BWD_TILE
    shards = tile // (2 * HALF)
    return pl.pallas_call(
        backward_kernel,
        grid_spec=pltpu.PrefetchScalarGridSpec(
            num_scalar_prefetch=1,
            grid=(width // tile,),
            in_specs=[
                pl.BlockSpec((groups * tokens, keys), lambda k, c: (0, 0)),
                pl.BlockSpec((shards, HALF, keys), lambda k, c: (k, 0, 0)),
                pl.BlockSpec((shards, HALF, keys), lambda k, c: (k, 0, 0)),
                pl.BlockSpec((tokens, tile), lambda k, c: (0, k)),
                pl.BlockSpec((tokens, 1), lambda k, c: (0, 0)),
            ],
            out_specs=pl.BlockSpec((groups, tile), lambda k, c: (0, k)),
        ),
        out_shape=jax.ShapeDtypeStruct((groups, width), jnp.float32),
        compiler_params=pltpu.CompilerParams(dimension_semantics=("arbitrary",)),
    )(core, back_rows, first, second, activations, inv_rms)


def per_device(activations, gain, key_weight, key_gain, cotangent, directions):
    tokens_dev = activations.shape[0]
    total_tokens = tokens_dev * lax.axis_size("dp") * lax.axis_size("fsdp")
    values = activations.astype(jnp.float32)
    inv_rms = 1.0 / jnp.sqrt(jnp.mean(values * values, axis=1, keepdims=True) + 1e-05)
    groups = directions.shape[1] + 1
    core = (lax.axis_index("dp") % 2).astype(jnp.int32).reshape(1)

    first, second, gd = gather_weight(key_weight, gain, directions)
    kg_row = jnp.tile(key_gain, HEADS_KV)[None, :]

    back_rows = forward_rows(core, activations, inv_rms, gd, first, second, cotangent, kg_row)
    partial_terms = backward_terms(core, back_rows, first, second, activations, inv_rms, groups)
    shared_rows = sum_at_owner(partial_terms, "fsdp", 1)
    summed = sum_over_pairs(shared_rows, "dp") / math.sqrt(total_tokens)
    images = summed[1:]
    gram_matrix = of_everyone(
        jnp.dot(images, images.T, precision=lax.Precision.HIGHEST), "fsdp"
    )
    factor = jnp.linalg.cholesky(gram_matrix)
    ortho_basis = math.sqrt(D) * jax.scipy.linalg.solve_triangular(factor, images, lower=True)
    return (ortho_basis.T, summed[0])


def solution(mesh):
    placed = (
        P(("dp", "fsdp"), None),
        P("fsdp"),
        P("fsdp", None),
        P(),
        P(("dp", "fsdp"), None),
        P("fsdp", None),
    )
    return jax.shard_map(
        per_device,
        mesh=mesh,
        in_specs=placed,
        out_specs=(P("fsdp", None), P("fsdp")),
        check_vma=False,
    )
```

```python
import math

import jax
import jax.numpy as jnp
from jax import lax
from jax.experimental import pallas as pl
from jax.experimental.pallas import tpu as pltpu
from jax.sharding import PartitionSpec as P

D = 8192
HEADS_KV = 4
HEAD_DIM = 128
HALF = 128
EXTRA_ROWS = 8
FWD_TILE = 1024
BWD_TILE = 1024


def in_blocks(shard, dim, devices):
    shape = shard.shape
    parts = shard.reshape(*shape[:dim], devices, shape[dim] // devices, *shape[dim + 1 :])
    return jnp.moveaxis(parts, dim, 0)


def sum_at_owner(shard, axis, dim):
    devices = lax.axis_size(axis)
    parts = lax.all_to_all(in_blocks(shard, dim, devices), axis, 0, 0, tiled=True)
    return jnp.sum(parts, axis=0)


def copy_for_each(shard, axis):
    copies = jnp.broadcast_to(shard, (lax.axis_size(axis), *shard.shape))
    return lax.all_to_all(copies, axis, split_axis=0, concat_axis=0, tiled=True)


def of_everyone(shard, axis):
    return copy_for_each(shard, axis).sum(axis=0)


def sum_over_pairs(shard, axis):
    devices = lax.axis_size(axis)
    step = 1
    while step < devices:
        shard = shard + lax.ppermute(shard, axis, [(i, i ^ step) for i in range(devices)])
        step *= 2
    return shard


def gather_weight(key_weight, gain, directions):
    rows, width = key_weight.shape
    half = rows // 2
    core = lax.axis_index("dp") % 2
    mine = lax.dynamic_slice_in_dim(key_weight, core * half, half, 0)
    extra = jnp.concatenate([gain[None, :], directions.T], axis=0)
    count = extra.shape[0]
    per_row = width // rows
    packed_rows = -(-count // per_row)
    extra = jnp.pad(extra, ((0, packed_rows * per_row - count), (0, 0)))
    extra = extra.reshape(packed_rows, width)
    extra = jnp.pad(extra, ((0, EXTRA_ROWS - packed_rows), (0, 0)))
    piece = jnp.concatenate([mine, extra], axis=0)
    first = copy_for_each(piece, "fsdp")
    dp = lax.axis_size("dp")
    second = lax.ppermute(first, "dp", [(i, i ^ 1) for i in range(dp)])
    devices = first.shape[0]
    extras = first[:, half : half + packed_rows, :].reshape(devices, packed_rows * per_row, rows)
    extras = jnp.transpose(extras[:, :count, :], (1, 0, 2)).reshape(count, -1)
    return first, second, extras.astype(jnp.float32)


def middle_rows(acc, cot, key_gain_row, back_ref):
    tokens = cot.shape[0]
    groups = acc.shape[0] // tokens
    weighted_all = cot.astype(jnp.float32) * key_gain_row
    for h in range(HEADS_KV):
        cols = slice(h * HEAD_DIM, (h + 1) * HEAD_DIM)
        key = acc[0:tokens, cols]
        weighted = weighted_all[:, cols]
        key_scale = jnp.sqrt(jnp.sum(key * key, axis=-1, keepdims=True) / HEAD_DIM + 1e-05)
        unit_keys = key / key_scale
        inner_sum = jnp.sum(unit_keys * weighted, axis=-1, keepdims=True)
        grad_keys = (weighted - unit_keys * inner_sum / HEAD_DIM) / key_scale
        back_ref[0:tokens, cols] = grad_keys.astype(back_ref.dtype)
        for j in range(1, groups):
            tangent = acc[j * tokens : (j + 1) * tokens, cols]
            shift_rate = jnp.sum(unit_keys * tangent, axis=-1, keepdims=True) / HEAD_DIM
            unit_change = (tangent - unit_keys * shift_rate) / key_scale
            along = jnp.sum(unit_change * weighted, axis=-1, keepdims=True)
            second = -(unit_change * inner_sum + unit_keys * along) / (
                HEAD_DIM * key_scale
            ) - grad_keys * shift_rate / key_scale
            back_ref[j * tokens : (j + 1) * tokens, cols] = second.astype(back_ref.dtype)


def build_lhs(act_ref, rms_ref, gd_ref, lhs_ref, offset):
    tokens = act_ref.shape[0]
    shard = 2 * HALF
    for g in range(act_ref.shape[1] // shard):
        cols = pl.ds(pl.multiple_of(g * shard + offset, HALF), HALF)
        normed = act_ref[:, cols].astype(jnp.float32) / rms_ref[...]
        gd = gd_ref[:, cols]
        for j in range(gd_ref.shape[0]):
            lhs_ref[j * tokens : (j + 1) * tokens, g * HALF : (g + 1) * HALF] = (
                normed * gd[j : j + 1, :]
            ).astype(jnp.bfloat16)


def build_for(core_ref, act_ref, rms_ref, gd_ref, lhs_ref, own):
    core = core_ref[0] if own else 1 - core_ref[0]
    build_lhs(act_ref, rms_ref, gd_ref, lhs_ref, core * HALF)


def weight_tile(w_ref):
    shards, rows, width = w_ref.shape
    return w_ref[...].reshape(shards * rows, width)


def forward_first_kernel(core_ref, act_ref, rms_ref, gd_ref, w_ref, out_ref, lhs_ref):
    k = pl.program_id(0)

    @pl.when(k == 0)
    def _():
        out_ref[...] = jnp.zeros_like(out_ref)

    build_for(core_ref, act_ref, rms_ref, gd_ref, lhs_ref, True)
    out_ref[...] += jnp.dot(lhs_ref[...], weight_tile(w_ref), preferred_element_type=jnp.float32)


def forward_second_kernel(
    core_ref, act_ref, rms_ref, gd_ref, w_ref, acc_in_ref, cot_ref, kg_ref, back_ref, lhs_ref, acc_ref
):
    k = pl.program_id(0)

    @pl.when(k == 0)
    def _():
        acc_ref[...] = acc_in_ref[...]

    build_for(core_ref, act_ref, rms_ref, gd_ref, lhs_ref, False)
    acc_ref[...] += jnp.dot(lhs_ref[...], weight_tile(w_ref), preferred_element_type=jnp.float32)

    @pl.when(k == pl.num_programs(0) - 1)
    def _():
        middle_rows(acc_ref[...], cot_ref[...], kg_ref[...], back_ref)


def forward_rows(core, activations, rms, gd, first, second, cot, kg_row):
    tokens, width = activations.shape
    groups = gd.shape[0]
    keys = first.shape[2]
    tile = 2 * FWD_TILE
    shards = tile // (2 * HALF)
    common = [
        pl.BlockSpec((tokens, tile), lambda k, c: (0, k)),
        pl.BlockSpec((tokens, 1), lambda k, c: (0, 0)),
        pl.BlockSpec((groups, tile), lambda k, c: (0, k)),
        pl.BlockSpec((shards, HALF, keys), lambda k, c: (k, 0, 0)),
    ]
    params = pltpu.CompilerParams(dimension_semantics=("arbitrary",))
    acc = pl.pallas_call(
        forward_first_kernel,
        grid_spec=pltpu.PrefetchScalarGridSpec(
            num_scalar_prefetch=1,
            grid=(width // tile,),
            in_specs=common,
            out_specs=pl.BlockSpec((groups * tokens, keys), lambda k, c: (0, 0)),
            scratch_shapes=[pltpu.VMEM((groups * tokens, FWD_TILE), jnp.bfloat16)],
        ),
        out_shape=jax.ShapeDtypeStruct((groups * tokens, keys), jnp.float32),
        compiler_params=params,
    )(core, activations, rms, gd, first)
    return pl.pallas_call(
        forward_second_kernel,
        grid_spec=pltpu.PrefetchScalarGridSpec(
            num_scalar_prefetch=1,
            grid=(width // tile,),
            in_specs=common
            + [
                pl.BlockSpec((groups * tokens, keys), lambda k, c: (0, 0)),
                pl.BlockSpec((tokens, keys), lambda k, c: (0, 0)),
                pl.BlockSpec((1, keys), lambda k, c: (0, 0)),
            ],
            out_specs=pl.BlockSpec((groups * tokens, keys), lambda k, c: (0, 0)),
            scratch_shapes=[
                pltpu.VMEM((groups * tokens, FWD_TILE), jnp.bfloat16),
                pltpu.VMEM((groups * tokens, keys), jnp.float32),
            ],
        ),
        out_shape=jax.ShapeDtypeStruct((groups * tokens, keys), jnp.bfloat16),
        compiler_params=params,
    )(core, activations, rms, gd, second, acc, cot, kg_row)


def backward_kernel(core_ref, back_ref, w1_ref, w2_ref, act_ref, rms_ref, out_ref):
    tokens = act_ref.shape[0]
    groups = out_ref.shape[0]
    shard = 2 * HALF

    def product_of(w_ref):
        return lax.dot_general(
            back_ref[...],
            weight_tile(w_ref),
            (((1,), (1,)), ((), ())),
            preferred_element_type=jnp.float32,
        )

    own = product_of(w1_ref)
    other = product_of(w2_ref)

    def emit(product, offset):
        for g in range(act_ref.shape[1] // shard):
            cols = pl.ds(pl.multiple_of(g * shard + offset, HALF), HALF)
            normed = act_ref[:, cols].astype(jnp.float32) / rms_ref[...]
            part = product[:, g * HALF : (g + 1) * HALF].reshape(groups, tokens, HALF)
            out_ref[:, cols] = jnp.sum(part * normed[None], axis=1)

    core = core_ref[0]
    emit(own, core * HALF)
    emit(other, (1 - core) * HALF)


def backward_terms(core, back_rows, first, second, activations, rms, groups):
    tokens, width = activations.shape
    keys = first.shape[2]
    tile = 2 * BWD_TILE
    shards = tile // (2 * HALF)
    return pl.pallas_call(
        backward_kernel,
        grid_spec=pltpu.PrefetchScalarGridSpec(
            num_scalar_prefetch=1,
            grid=(width // tile,),
            in_specs=[
                pl.BlockSpec((groups * tokens, keys), lambda k, c: (0, 0)),
                pl.BlockSpec((shards, HALF, keys), lambda k, c: (k, 0, 0)),
                pl.BlockSpec((shards, HALF, keys), lambda k, c: (k, 0, 0)),
                pl.BlockSpec((tokens, tile), lambda k, c: (0, k)),
                pl.BlockSpec((tokens, 1), lambda k, c: (0, 0)),
            ],
            out_specs=pl.BlockSpec((groups, tile), lambda k, c: (0, k)),
        ),
        out_shape=jax.ShapeDtypeStruct((groups, width), jnp.float32),
        compiler_params=pltpu.CompilerParams(dimension_semantics=("arbitrary",)),
    )(core, back_rows, first, second, activations, rms)


def per_device(activations, gain, key_weight, key_gain, cotangent, directions):
    tokens_dev = activations.shape[0]
    total_tokens = tokens_dev * lax.axis_size("dp") * lax.axis_size("fsdp")
    values = activations.astype(jnp.float32)
    rms = jnp.sqrt(jnp.mean(values * values, axis=1, keepdims=True) + 1e-05)
    groups = directions.shape[1] + 1
    core = (lax.axis_index("dp") % 2).astype(jnp.int32).reshape(1)

    first, second, gd = gather_weight(key_weight, gain, directions)
    kg_row = jnp.tile(key_gain, HEADS_KV)[None, :]

    back_rows = forward_rows(core, activations, rms, gd, first, second, cotangent, kg_row)
    partial_terms = backward_terms(core, back_rows, first, second, activations, rms, groups)
    shared_rows = sum_at_owner(partial_terms, "fsdp", 1)
    summed = sum_over_pairs(shared_rows, "dp") / math.sqrt(total_tokens)
    images = summed[1:]
    gram_matrix = of_everyone(
        jnp.dot(images, images.T, precision=lax.Precision.HIGHEST), "fsdp"
    )
    factor = jnp.linalg.cholesky(gram_matrix)
    ortho_basis = math.sqrt(D) * jax.scipy.linalg.solve_triangular(factor, images, lower=True)
    return (ortho_basis.T, summed[0])


def solution(mesh):
    placed = (
        P(("dp", "fsdp"), None),
        P("fsdp"),
        P("fsdp", None),
        P(),
        P(("dp", "fsdp"), None),
        P("fsdp", None),
    )
    return jax.shard_map(
        per_device,
        mesh=mesh,
        in_specs=placed,
        out_specs=(P("fsdp", None), P("fsdp")),
        check_vma=False,
    )
```

```python
import math

import jax
import jax.numpy as jnp
from jax import lax
from jax.experimental import pallas as pl
from jax.experimental.pallas import tpu as pltpu
from jax.sharding import PartitionSpec as P

D = 8192
HEADS_KV = 4
HEAD_DIM = 128
HALF = 128
EXTRA_ROWS = 8
SUBS = 2
FWD_TILE = 1024
BWD_TILE = 1024


def in_blocks(shard, dim, devices):
    shape = shard.shape
    parts = shard.reshape(*shape[:dim], devices, shape[dim] // devices, *shape[dim + 1 :])
    return jnp.moveaxis(parts, dim, 0)


def sum_at_owner(shard, axis, dim):
    devices = lax.axis_size(axis)
    parts = lax.all_to_all(in_blocks(shard, dim, devices), axis, 0, 0, tiled=True)
    return jnp.sum(parts, axis=0)


def copy_for_each(shard, axis):
    copies = jnp.broadcast_to(shard, (lax.axis_size(axis), *shard.shape))
    return lax.all_to_all(copies, axis, split_axis=0, concat_axis=0, tiled=True)


def of_everyone(shard, axis):
    return copy_for_each(shard, axis).sum(axis=0)


def sum_over_pairs(shard, axis):
    devices = lax.axis_size(axis)
    step = 1
    while step < devices:
        shard = shard + lax.ppermute(shard, axis, [(i, i ^ step) for i in range(devices)])
        step *= 2
    return shard


def gather_weight(key_weight, gain, directions):
    rows, width = key_weight.shape
    half = rows // 2
    core = lax.axis_index("dp") % 2
    mine = lax.dynamic_slice_in_dim(key_weight, core * half, half, 0)
    extra = jnp.concatenate([gain[None, :], directions.T], axis=0)
    count = extra.shape[0]
    per_row = width // rows
    packed_rows = -(-count // per_row)
    extra = jnp.pad(extra, ((0, packed_rows * per_row - count), (0, 0)))
    extra = extra.reshape(packed_rows, width)
    extra = jnp.pad(extra, ((0, EXTRA_ROWS - packed_rows), (0, 0)))
    piece = jnp.concatenate([mine, extra], axis=0)
    first = copy_for_each(piece, "fsdp")
    dp = lax.axis_size("dp")
    second = lax.ppermute(first, "dp", [(i, i ^ 1) for i in range(dp)])
    devices = first.shape[0]
    extras = first[:, half : half + packed_rows, :].reshape(devices, packed_rows * per_row, rows)
    extras = jnp.transpose(extras[:, :count, :], (1, 0, 2)).reshape(count, -1)
    return first, second, extras.astype(jnp.float32)


def middle_rows(acc, cot, key_gain_row, back_ref):
    tokens = cot.shape[0]
    groups = acc.shape[0] // tokens
    weighted_all = cot.astype(jnp.float32) * key_gain_row
    for h in range(HEADS_KV):
        cols = slice(h * HEAD_DIM, (h + 1) * HEAD_DIM)
        key = acc[0:tokens, cols]
        weighted = weighted_all[:, cols]
        key_scale = jnp.sqrt(jnp.sum(key * key, axis=-1, keepdims=True) / HEAD_DIM + 1e-05)
        unit_keys = key / key_scale
        inner_sum = jnp.sum(unit_keys * weighted, axis=-1, keepdims=True)
        grad_keys = (weighted - unit_keys * inner_sum / HEAD_DIM) / key_scale
        back_ref[0:tokens, cols] = grad_keys.astype(back_ref.dtype)
        for j in range(1, groups):
            tangent = acc[j * tokens : (j + 1) * tokens, cols]
            shift_rate = jnp.sum(unit_keys * tangent, axis=-1, keepdims=True) / HEAD_DIM
            unit_change = (tangent - unit_keys * shift_rate) / key_scale
            along = jnp.sum(unit_change * weighted, axis=-1, keepdims=True)
            second = -(unit_change * inner_sum + unit_keys * along) / (
                HEAD_DIM * key_scale
            ) - grad_keys * shift_rate / key_scale
            back_ref[j * tokens : (j + 1) * tokens, cols] = second.astype(back_ref.dtype)


def build_lhs(act_ref, rms_ref, gd_ref, lhs_ref, offset, sub, shards):
    tokens = act_ref.shape[0]
    shard = 2 * HALF
    for n in range(shards):
        g = sub * shards + n
        cols = pl.ds(pl.multiple_of(g * shard + offset, HALF), HALF)
        normed = act_ref[:, cols].astype(jnp.float32) / rms_ref[...]
        gd = gd_ref[:, cols]
        for j in range(gd_ref.shape[0]):
            lhs_ref[sub, j * tokens : (j + 1) * tokens, n * HALF : (n + 1) * HALF] = (
                normed * gd[j : j + 1, :]
            ).astype(jnp.bfloat16)


def forward_step(core_ref, act_ref, rms_ref, gd_ref, w_ref, lhs_ref, own):
    core = core_ref[0] if own else 1 - core_ref[0]
    subs = lhs_ref.shape[0]
    shards = w_ref.shape[0] // subs
    total = None
    for sub in range(subs):
        build_lhs(act_ref, rms_ref, gd_ref, lhs_ref, core * HALF, sub, shards)
        w = w_ref[sub * shards : (sub + 1) * shards]
        w = w.reshape(shards * w.shape[1], w.shape[2])
        part = jnp.dot(lhs_ref[sub], w, preferred_element_type=jnp.float32)
        total = part if total is None else total + part
    return total


def weight_tile(w_ref):
    shards, rows, width = w_ref.shape
    return w_ref[...].reshape(shards * rows, width)


def forward_first_kernel(core_ref, act_ref, rms_ref, gd_ref, w_ref, out_ref, lhs_ref):
    k = pl.program_id(0)

    @pl.when(k == 0)
    def _():
        out_ref[...] = jnp.zeros_like(out_ref)

    out_ref[...] += forward_step(core_ref, act_ref, rms_ref, gd_ref, w_ref, lhs_ref, True)


def forward_second_kernel(
    core_ref, act_ref, rms_ref, gd_ref, w_ref, acc_in_ref, cot_ref, kg_ref, back_ref, lhs_ref, acc_ref
):
    k = pl.program_id(0)

    @pl.when(k == 0)
    def _():
        acc_ref[...] = acc_in_ref[...]

    acc_ref[...] += forward_step(core_ref, act_ref, rms_ref, gd_ref, w_ref, lhs_ref, False)

    @pl.when(k == pl.num_programs(0) - 1)
    def _():
        middle_rows(acc_ref[...], cot_ref[...], kg_ref[...], back_ref)


def forward_rows(core, activations, rms, gd, first, second, cot, kg_row):
    tokens, width = activations.shape
    groups = gd.shape[0]
    keys = first.shape[2]
    tile = 2 * FWD_TILE
    shards = tile // (2 * HALF)
    common = [
        pl.BlockSpec((tokens, tile), lambda k, c: (0, k)),
        pl.BlockSpec((tokens, 1), lambda k, c: (0, 0)),
        pl.BlockSpec((groups, tile), lambda k, c: (0, k)),
        pl.BlockSpec((shards, HALF, keys), lambda k, c: (k, 0, 0)),
    ]
    params = pltpu.CompilerParams(dimension_semantics=("arbitrary",))
    acc = pl.pallas_call(
        forward_first_kernel,
        grid_spec=pltpu.PrefetchScalarGridSpec(
            num_scalar_prefetch=1,
            grid=(width // tile,),
            in_specs=common,
            out_specs=pl.BlockSpec((groups * tokens, keys), lambda k, c: (0, 0)),
            scratch_shapes=[pltpu.VMEM((SUBS, groups * tokens, FWD_TILE // SUBS), jnp.bfloat16)],
        ),
        out_shape=jax.ShapeDtypeStruct((groups * tokens, keys), jnp.float32),
        compiler_params=params,
    )(core, activations, rms, gd, first)
    return pl.pallas_call(
        forward_second_kernel,
        grid_spec=pltpu.PrefetchScalarGridSpec(
            num_scalar_prefetch=1,
            grid=(width // tile,),
            in_specs=common
            + [
                pl.BlockSpec((groups * tokens, keys), lambda k, c: (0, 0)),
                pl.BlockSpec((tokens, keys), lambda k, c: (0, 0)),
                pl.BlockSpec((1, keys), lambda k, c: (0, 0)),
            ],
            out_specs=pl.BlockSpec((groups * tokens, keys), lambda k, c: (0, 0)),
            scratch_shapes=[
                pltpu.VMEM((SUBS, groups * tokens, FWD_TILE // SUBS), jnp.bfloat16),
                pltpu.VMEM((groups * tokens, keys), jnp.float32),
            ],
        ),
        out_shape=jax.ShapeDtypeStruct((groups * tokens, keys), jnp.bfloat16),
        compiler_params=params,
    )(core, activations, rms, gd, second, acc, cot, kg_row)


def backward_kernel(core_ref, back_ref, w1_ref, w2_ref, act_ref, rms_ref, out_ref):
    tokens = act_ref.shape[0]
    groups = out_ref.shape[0]
    shard = 2 * HALF

    def product_of(w_ref):
        return lax.dot_general(
            back_ref[...],
            weight_tile(w_ref),
            (((1,), (1,)), ((), ())),
            preferred_element_type=jnp.float32,
        )

    own = product_of(w1_ref)
    other = product_of(w2_ref)

    def emit(product, offset):
        for g in range(act_ref.shape[1] // shard):
            cols = pl.ds(pl.multiple_of(g * shard + offset, HALF), HALF)
            normed = act_ref[:, cols].astype(jnp.float32) / rms_ref[...]
            part = product[:, g * HALF : (g + 1) * HALF].reshape(groups, tokens, HALF)
            out_ref[:, cols] = jnp.sum(part * normed[None], axis=1)

    core = core_ref[0]
    emit(own, core * HALF)
    emit(other, (1 - core) * HALF)


def backward_terms(core, back_rows, first, second, activations, rms, groups):
    tokens, width = activations.shape
    keys = first.shape[2]
    tile = 2 * BWD_TILE
    shards = tile // (2 * HALF)
    return pl.pallas_call(
        backward_kernel,
        grid_spec=pltpu.PrefetchScalarGridSpec(
            num_scalar_prefetch=1,
            grid=(width // tile,),
            in_specs=[
                pl.BlockSpec((groups * tokens, keys), lambda k, c: (0, 0)),
                pl.BlockSpec((shards, HALF, keys), lambda k, c: (k, 0, 0)),
                pl.BlockSpec((shards, HALF, keys), lambda k, c: (k, 0, 0)),
                pl.BlockSpec((tokens, tile), lambda k, c: (0, k)),
                pl.BlockSpec((tokens, 1), lambda k, c: (0, 0)),
            ],
            out_specs=pl.BlockSpec((groups, tile), lambda k, c: (0, k)),
        ),
        out_shape=jax.ShapeDtypeStruct((groups, width), jnp.float32),
        compiler_params=pltpu.CompilerParams(dimension_semantics=("arbitrary",)),
    )(core, back_rows, first, second, activations, rms)


def per_device(activations, gain, key_weight, key_gain, cotangent, directions):
    tokens_dev = activations.shape[0]
    total_tokens = tokens_dev * lax.axis_size("dp") * lax.axis_size("fsdp")
    values = activations.astype(jnp.float32)
    rms = jnp.sqrt(jnp.mean(values * values, axis=1, keepdims=True) + 1e-05)
    groups = directions.shape[1] + 1
    core = (lax.axis_index("dp") % 2).astype(jnp.int32).reshape(1)

    first, second, gd = gather_weight(key_weight, gain, directions)
    kg_row = jnp.tile(key_gain, HEADS_KV)[None, :]

    back_rows = forward_rows(core, activations, rms, gd, first, second, cotangent, kg_row)
    partial_terms = backward_terms(core, back_rows, first, second, activations, rms, groups)
    shared_rows = sum_at_owner(partial_terms, "fsdp", 1)
    summed = sum_over_pairs(shared_rows, "dp") / math.sqrt(total_tokens)
    images = summed[1:]
    gram_matrix = of_everyone(
        jnp.dot(images, images.T, precision=lax.Precision.HIGHEST), "fsdp"
    )
    factor = jnp.linalg.cholesky(gram_matrix)
    ortho_basis = math.sqrt(D) * jax.scipy.linalg.solve_triangular(factor, images, lower=True)
    return (ortho_basis.T, summed[0])


def solution(mesh):
    placed = (
        P(("dp", "fsdp"), None),
        P("fsdp"),
        P("fsdp", None),
        P(),
        P(("dp", "fsdp"), None),
        P("fsdp", None),
    )
    return jax.shard_map(
        per_device,
        mesh=mesh,
        in_specs=placed,
        out_specs=(P("fsdp", None), P("fsdp")),
        check_vma=False,
    )
```

```python
import math

import jax
import jax.numpy as jnp
from jax import lax
from jax.experimental import pallas as pl
from jax.experimental.pallas import tpu as pltpu
from jax.sharding import PartitionSpec as P

D = 8192
HEADS_KV = 4
HEAD_DIM = 128
HALF = 128
EXTRA_ROWS = 8
GROUPS = 9
FWD_TILE = 1024
BWD_TILE = 1024


def in_blocks(shard, dim, devices):
    shape = shard.shape
    parts = shard.reshape(*shape[:dim], devices, shape[dim] // devices, *shape[dim + 1 :])
    return jnp.moveaxis(parts, dim, 0)


def sum_at_owner(shard, axis, dim):
    devices = lax.axis_size(axis)
    parts = lax.all_to_all(in_blocks(shard, dim, devices), axis, 0, 0, tiled=True)
    return jnp.sum(parts, axis=0)


def copy_for_each(shard, axis):
    copies = jnp.broadcast_to(shard, (lax.axis_size(axis), *shard.shape))
    return lax.all_to_all(copies, axis, split_axis=0, concat_axis=0, tiled=True)


def of_everyone(shard, axis):
    return copy_for_each(shard, axis).sum(axis=0)


def sum_over_pairs(shard, axis):
    devices = lax.axis_size(axis)
    step = 1
    while step < devices:
        shard = shard + lax.ppermute(shard, axis, [(i, i ^ step) for i in range(devices)])
        step *= 2
    return shard


def gather_weight(key_weight, gain, directions):
    rows, width = key_weight.shape
    half = rows // 2
    core = lax.axis_index("dp") % 2
    mine = lax.dynamic_slice_in_dim(key_weight, core * half, half, 0)
    extra = jnp.concatenate([gain[None, :], directions.T], axis=0)
    count = extra.shape[0]
    per_row = width // rows
    packed_rows = -(-count // per_row)
    extra = jnp.pad(extra, ((0, packed_rows * per_row - count), (0, 0)))
    extra = extra.reshape(packed_rows, width)
    extra = jnp.pad(extra, ((0, EXTRA_ROWS - packed_rows), (0, 0)))
    piece = jnp.concatenate([mine, extra], axis=0)
    first = copy_for_each(piece, "fsdp")
    dp = lax.axis_size("dp")
    second = lax.ppermute(first, "dp", [(i, i ^ 1) for i in range(dp)])
    return first, second


def middle_rows(acc, cot, key_gain_row, back_ref):
    tokens = cot.shape[0]
    groups = acc.shape[0] // tokens
    weighted_all = cot.astype(jnp.float32) * key_gain_row
    for h in range(HEADS_KV):
        cols = slice(h * HEAD_DIM, (h + 1) * HEAD_DIM)
        key = acc[0:tokens, cols]
        weighted = weighted_all[:, cols]
        key_scale = jnp.sqrt(jnp.sum(key * key, axis=-1, keepdims=True) / HEAD_DIM + 1e-05)
        unit_keys = key / key_scale
        inner_sum = jnp.sum(unit_keys * weighted, axis=-1, keepdims=True)
        grad_keys = (weighted - unit_keys * inner_sum / HEAD_DIM) / key_scale
        back_ref[0:tokens, cols] = grad_keys.astype(back_ref.dtype)
        for j in range(1, groups):
            tangent = acc[j * tokens : (j + 1) * tokens, cols]
            shift_rate = jnp.sum(unit_keys * tangent, axis=-1, keepdims=True) / HEAD_DIM
            unit_change = (tangent - unit_keys * shift_rate) / key_scale
            along = jnp.sum(unit_change * weighted, axis=-1, keepdims=True)
            second = -(unit_change * inner_sum + unit_keys * along) / (
                HEAD_DIM * key_scale
            ) - grad_keys * shift_rate / key_scale
            back_ref[j * tokens : (j + 1) * tokens, cols] = second.astype(back_ref.dtype)


def build_lhs(act_ref, rms_ref, ext_ref, lhs_ref, offset):
    tokens = act_ref.shape[0]
    shard = 2 * HALF
    per_row = ext_ref.shape[2] // shard
    for g in range(act_ref.shape[1] // shard):
        cols = pl.ds(pl.multiple_of(g * shard + offset, HALF), HALF)
        normed = act_ref[:, cols].astype(jnp.float32) / rms_ref[...]
        for j in range(GROUPS):
            lanes = pl.ds(pl.multiple_of((j % per_row) * shard + offset, HALF), HALF)
            scale = ext_ref[g, pl.ds(j // per_row, 1), lanes].astype(jnp.float32)
            lhs_ref[j * tokens : (j + 1) * tokens, g * HALF : (g + 1) * HALF] = (
                normed * scale
            ).astype(jnp.bfloat16)


def build_for(core_ref, act_ref, rms_ref, ext_ref, lhs_ref, own):
    core = core_ref[0] if own else 1 - core_ref[0]
    build_lhs(act_ref, rms_ref, ext_ref, lhs_ref, core * HALF)


def weight_tile(w_ref):
    shards, rows, width = w_ref.shape
    return w_ref[...].reshape(shards * rows, width)


def forward_first_kernel(core_ref, act_ref, rms_ref, gd_ref, w_ref, out_ref, lhs_ref):
    k = pl.program_id(0)

    @pl.when(k == 0)
    def _():
        out_ref[...] = jnp.zeros_like(out_ref)

    build_for(core_ref, act_ref, rms_ref, gd_ref, lhs_ref, True)
    out_ref[...] += jnp.dot(lhs_ref[...], weight_tile(w_ref), preferred_element_type=jnp.float32)


def forward_second_kernel(
    core_ref, act_ref, rms_ref, gd_ref, w_ref, acc_in_ref, cot_ref, kg_ref, back_ref, lhs_ref, acc_ref
):
    k = pl.program_id(0)

    @pl.when(k == 0)
    def _():
        acc_ref[...] = acc_in_ref[...]

    build_for(core_ref, act_ref, rms_ref, gd_ref, lhs_ref, False)
    acc_ref[...] += jnp.dot(lhs_ref[...], weight_tile(w_ref), preferred_element_type=jnp.float32)

    @pl.when(k == pl.num_programs(0) - 1)
    def _():
        middle_rows(acc_ref[...], cot_ref[...], kg_ref[...], back_ref)


def forward_rows(core, activations, rms, first, second, cot, kg_row):
    tokens, width = activations.shape
    groups = GROUPS
    keys = first.shape[2]
    tile = 2 * FWD_TILE
    shards = tile // (2 * HALF)
    common = [
        pl.BlockSpec((tokens, tile), lambda k, c: (0, k)),
        pl.BlockSpec((tokens, 1), lambda k, c: (0, 0)),
        pl.BlockSpec((shards, EXTRA_ROWS, keys), lambda k, c: (k, HALF // EXTRA_ROWS, 0)),
        pl.BlockSpec((shards, HALF, keys), lambda k, c: (k, 0, 0)),
    ]
    params = pltpu.CompilerParams(dimension_semantics=("arbitrary",))
    acc = pl.pallas_call(
        forward_first_kernel,
        grid_spec=pltpu.PrefetchScalarGridSpec(
            num_scalar_prefetch=1,
            grid=(width // tile,),
            in_specs=common,
            out_specs=pl.BlockSpec((groups * tokens, keys), lambda k, c: (0, 0)),
            scratch_shapes=[pltpu.VMEM((groups * tokens, FWD_TILE), jnp.bfloat16)],
        ),
        out_shape=jax.ShapeDtypeStruct((groups * tokens, keys), jnp.float32),
        compiler_params=params,
    )(core, activations, rms, first, first)
    return pl.pallas_call(
        forward_second_kernel,
        grid_spec=pltpu.PrefetchScalarGridSpec(
            num_scalar_prefetch=1,
            grid=(width // tile,),
            in_specs=common
            + [
                pl.BlockSpec((groups * tokens, keys), lambda k, c: (0, 0)),
                pl.BlockSpec((tokens, keys), lambda k, c: (0, 0)),
                pl.BlockSpec((1, keys), lambda k, c: (0, 0)),
            ],
            out_specs=pl.BlockSpec((groups * tokens, keys), lambda k, c: (0, 0)),
            scratch_shapes=[
                pltpu.VMEM((groups * tokens, FWD_TILE), jnp.bfloat16),
                pltpu.VMEM((groups * tokens, keys), jnp.float32),
            ],
        ),
        out_shape=jax.ShapeDtypeStruct((groups * tokens, keys), jnp.bfloat16),
        compiler_params=params,
    )(core, activations, rms, first, second, acc, cot, kg_row)


def backward_kernel(core_ref, back_ref, w1_ref, w2_ref, act_ref, rms_ref, out_ref):
    tokens = act_ref.shape[0]
    groups = out_ref.shape[1]
    shard = 2 * HALF

    def product_of(w_ref):
        return lax.dot_general(
            back_ref[...],
            weight_tile(w_ref),
            (((1,), (1,)), ((), ())),
            preferred_element_type=jnp.float32,
        )

    own = product_of(w1_ref)
    other = product_of(w2_ref)

    def emit(product, offset):
        for g in range(act_ref.shape[1] // shard):
            cols = pl.ds(pl.multiple_of(g * shard + offset, HALF), HALF)
            normed = act_ref[:, cols].astype(jnp.float32) / rms_ref[...]
            part = product[:, g * HALF : (g + 1) * HALF].reshape(groups, tokens, HALF)
            out_ref[g, :, pl.ds(pl.multiple_of(offset, HALF), HALF)] = jnp.sum(
                part * normed[None], axis=1
            )

    core = core_ref[0]
    emit(own, core * HALF)
    emit(other, (1 - core) * HALF)


def backward_terms(core, back_rows, first, second, activations, rms, groups):
    tokens, width = activations.shape
    keys = first.shape[2]
    tile = 2 * BWD_TILE
    shards = tile // (2 * HALF)
    return pl.pallas_call(
        backward_kernel,
        grid_spec=pltpu.PrefetchScalarGridSpec(
            num_scalar_prefetch=1,
            grid=(width // tile,),
            in_specs=[
                pl.BlockSpec((groups * tokens, keys), lambda k, c: (0, 0)),
                pl.BlockSpec((shards, HALF, keys), lambda k, c: (k, 0, 0)),
                pl.BlockSpec((shards, HALF, keys), lambda k, c: (k, 0, 0)),
                pl.BlockSpec((tokens, tile), lambda k, c: (0, k)),
                pl.BlockSpec((tokens, 1), lambda k, c: (0, 0)),
            ],
            out_specs=pl.BlockSpec((shards, groups, 2 * HALF), lambda k, c: (k, 0, 0)),
        ),
        out_shape=jax.ShapeDtypeStruct((width // (2 * HALF), groups, 2 * HALF), jnp.float32),
        compiler_params=pltpu.CompilerParams(dimension_semantics=("arbitrary",)),
    )(core, back_rows, first, second, activations, rms)


def per_device(activations, gain, key_weight, key_gain, cotangent, directions):
    tokens_dev = activations.shape[0]
    total_tokens = tokens_dev * lax.axis_size("dp") * lax.axis_size("fsdp")
    values = activations.astype(jnp.float32)
    rms = jnp.sqrt(jnp.mean(values * values, axis=1, keepdims=True) + 1e-05)
    groups = directions.shape[1] + 1
    core = (lax.axis_index("dp") % 2).astype(jnp.int32).reshape(1)

    first, second = gather_weight(key_weight, gain, directions)
    kg_row = jnp.tile(key_gain, HEADS_KV)[None, :]

    back_rows = forward_rows(core, activations, rms, first, second, cotangent, kg_row)
    partial_terms = backward_terms(core, back_rows, first, second, activations, rms, groups)
    shared_rows = jnp.sum(lax.all_to_all(partial_terms, "fsdp", 0, 0, tiled=True), axis=0)
    summed = sum_over_pairs(shared_rows, "dp") / math.sqrt(total_tokens)
    images = summed[1:]
    gram_matrix = of_everyone(
        jnp.dot(images, images.T, precision=lax.Precision.HIGHEST), "fsdp"
    )
    factor = jnp.linalg.cholesky(gram_matrix)
    ortho_basis = math.sqrt(D) * jax.scipy.linalg.solve_triangular(factor, images, lower=True)
    return (ortho_basis.T, summed[0])


def solution(mesh):
    placed = (
        P(("dp", "fsdp"), None),
        P("fsdp"),
        P("fsdp", None),
        P(),
        P(("dp", "fsdp"), None),
        P("fsdp", None),
    )
    return jax.shard_map(
        per_device,
        mesh=mesh,
        in_specs=placed,
        out_specs=(P("fsdp", None), P("fsdp")),
        check_vma=False,
    )
```

```python
import math

import jax
import jax.numpy as jnp
from jax import lax
from jax.experimental import pallas as pl
from jax.experimental.pallas import tpu as pltpu
from jax.sharding import PartitionSpec as P

D = 8192
HEADS_KV = 4
HEAD_DIM = 128
HALF = 128
EXTRA_ROWS = 8
GROUPS = 9
FWD_TILE = 1024
BWD_TILE = 1024


def in_blocks(shard, dim, devices):
    shape = shard.shape
    parts = shard.reshape(*shape[:dim], devices, shape[dim] // devices, *shape[dim + 1 :])
    return jnp.moveaxis(parts, dim, 0)


def sum_at_owner(shard, axis, dim):
    devices = lax.axis_size(axis)
    parts = lax.all_to_all(in_blocks(shard, dim, devices), axis, 0, 0, tiled=True)
    return jnp.sum(parts, axis=0)


def copy_for_each(shard, axis):
    copies = jnp.broadcast_to(shard, (lax.axis_size(axis), *shard.shape))
    return lax.all_to_all(copies, axis, split_axis=0, concat_axis=0, tiled=True)


def of_everyone(shard, axis):
    return copy_for_each(shard, axis).sum(axis=0)


def sum_over_pairs(shard, axis):
    devices = lax.axis_size(axis)
    step = 1
    while step < devices:
        shard = shard + lax.ppermute(shard, axis, [(i, i ^ step) for i in range(devices)])
        step *= 2
    return shard


def gather_weight(key_weight, gain, directions):
    rows, width = key_weight.shape
    half = rows // 2
    core = lax.axis_index("dp") % 2
    mine = lax.dynamic_slice_in_dim(key_weight, core * half, half, 0)
    extra = jnp.concatenate([gain[None, :], directions.T], axis=0)
    count = extra.shape[0]
    per_row = width // rows
    packed_rows = -(-count // per_row)
    extra = jnp.pad(extra, ((0, packed_rows * per_row - count), (0, 0)))
    extra = extra.reshape(packed_rows, width)
    extra = jnp.pad(extra, ((0, EXTRA_ROWS - packed_rows), (0, 0)))
    piece = jnp.concatenate([mine, extra], axis=0)
    first = copy_for_each(piece, "fsdp")
    dp = lax.axis_size("dp")
    second = lax.ppermute(first, "dp", [(i, i ^ 1) for i in range(dp)])
    return first, second


def middle_rows(acc, cot, key_gain_row, back_ref):
    tokens = cot.shape[0]
    groups = acc.shape[0] // tokens
    for h in range(HEADS_KV):
        cols = slice(h * HEAD_DIM, (h + 1) * HEAD_DIM)
        key = acc[0:tokens, cols]
        weighted = cot[:, cols].astype(jnp.float32) * key_gain_row
        key_scale = jnp.sqrt(jnp.sum(key * key, axis=-1, keepdims=True) / HEAD_DIM + 1e-05)
        unit_keys = key / key_scale
        inner_sum = jnp.sum(unit_keys * weighted, axis=-1, keepdims=True)
        grad_keys = (weighted - unit_keys * inner_sum / HEAD_DIM) / key_scale
        back_ref[0:tokens, cols] = grad_keys.astype(back_ref.dtype)
        for j in range(1, groups):
            tangent = acc[j * tokens : (j + 1) * tokens, cols]
            shift_rate = jnp.sum(unit_keys * tangent, axis=-1, keepdims=True) / HEAD_DIM
            unit_change = (tangent - unit_keys * shift_rate) / key_scale
            along = jnp.sum(unit_change * weighted, axis=-1, keepdims=True)
            second = -(unit_change * inner_sum + unit_keys * along) / (
                HEAD_DIM * key_scale
            ) - grad_keys * shift_rate / key_scale
            back_ref[j * tokens : (j + 1) * tokens, cols] = second.astype(back_ref.dtype)


def build_lhs(act_ref, rms_ref, ext_ref, lhs_ref, offset):
    tokens = act_ref.shape[0]
    shard = 2 * HALF
    per_row = ext_ref.shape[2] // shard
    for g in range(act_ref.shape[1] // shard):
        cols = pl.ds(pl.multiple_of(g * shard + offset, HALF), HALF)
        normed = act_ref[:, cols].astype(jnp.float32) / rms_ref[...]
        for j in range(GROUPS):
            lanes = pl.ds(pl.multiple_of((j % per_row) * shard + offset, HALF), HALF)
            scale = ext_ref[g, pl.ds(j // per_row, 1), lanes].astype(jnp.float32)
            lhs_ref[j * tokens : (j + 1) * tokens, g * HALF : (g + 1) * HALF] = (
                normed * scale
            ).astype(jnp.bfloat16)


def build_for(core_ref, act_ref, rms_ref, ext_ref, lhs_ref, own):
    core = core_ref[0] if own else 1 - core_ref[0]
    build_lhs(act_ref, rms_ref, ext_ref, lhs_ref, core * HALF)


def weight_tile(w_ref):
    shards, rows, width = w_ref.shape
    return w_ref[...].reshape(shards * rows, width)


def forward_first_kernel(core_ref, act_ref, rms_ref, gd_ref, w_ref, out_ref, lhs_ref):
    k = pl.program_id(0)

    @pl.when(k == 0)
    def _():
        out_ref[...] = jnp.zeros_like(out_ref)

    build_for(core_ref, act_ref, rms_ref, gd_ref, lhs_ref, True)
    out_ref[...] += jnp.dot(lhs_ref[...], weight_tile(w_ref), preferred_element_type=jnp.float32)


def forward_second_kernel(
    core_ref, act_ref, rms_ref, gd_ref, w_ref, acc_in_ref, cot_ref, kg_ref, back_ref, lhs_ref, acc_ref
):
    k = pl.program_id(0)

    @pl.when(k == 0)
    def _():
        acc_ref[...] = acc_in_ref[...]

    build_for(core_ref, act_ref, rms_ref, gd_ref, lhs_ref, False)
    acc_ref[...] += jnp.dot(lhs_ref[...], weight_tile(w_ref), preferred_element_type=jnp.float32)

    @pl.when(k == pl.num_programs(0) - 1)
    def _():
        middle_rows(acc_ref[...], cot_ref[...], kg_ref[...], back_ref)


def forward_rows(core, activations, rms, first, second, cot, kg_row):
    tokens, width = activations.shape
    groups = GROUPS
    keys = first.shape[2]
    tile = 2 * FWD_TILE
    shards = tile // (2 * HALF)
    common = [
        pl.BlockSpec((tokens, tile), lambda k, c: (0, k)),
        pl.BlockSpec((tokens, HALF), lambda k, c: (0, 0)),
        pl.BlockSpec((shards, EXTRA_ROWS, keys), lambda k, c: (k, HALF // EXTRA_ROWS, 0)),
        pl.BlockSpec((shards, HALF, keys), lambda k, c: (k, 0, 0)),
    ]
    params = pltpu.CompilerParams(dimension_semantics=("arbitrary",))
    acc = pl.pallas_call(
        forward_first_kernel,
        grid_spec=pltpu.PrefetchScalarGridSpec(
            num_scalar_prefetch=1,
            grid=(width // tile,),
            in_specs=common,
            out_specs=pl.BlockSpec((groups * tokens, keys), lambda k, c: (0, 0)),
            scratch_shapes=[pltpu.VMEM((groups * tokens, FWD_TILE), jnp.bfloat16)],
        ),
        out_shape=jax.ShapeDtypeStruct((groups * tokens, keys), jnp.float32),
        compiler_params=params,
    )(core, activations, rms, first, first)
    return pl.pallas_call(
        forward_second_kernel,
        grid_spec=pltpu.PrefetchScalarGridSpec(
            num_scalar_prefetch=1,
            grid=(width // tile,),
            in_specs=common
            + [
                pl.BlockSpec((groups * tokens, keys), lambda k, c: (0, 0)),
                pl.BlockSpec((tokens, keys), lambda k, c: (0, 0)),
                pl.BlockSpec((1, HEAD_DIM), lambda k, c: (0, 0)),
            ],
            out_specs=pl.BlockSpec((groups * tokens, keys), lambda k, c: (0, 0)),
            scratch_shapes=[
                pltpu.VMEM((groups * tokens, FWD_TILE), jnp.bfloat16),
                pltpu.VMEM((groups * tokens, keys), jnp.float32),
            ],
        ),
        out_shape=jax.ShapeDtypeStruct((groups * tokens, keys), jnp.bfloat16),
        compiler_params=params,
    )(core, activations, rms, first, second, acc, cot, kg_row)


def backward_kernel(core_ref, back_ref, w1_ref, w2_ref, act_ref, rms_ref, out_ref):
    tokens = act_ref.shape[0]
    groups = out_ref.shape[1]
    shard = 2 * HALF

    def product_of(w_ref):
        return lax.dot_general(
            back_ref[...],
            weight_tile(w_ref),
            (((1,), (1,)), ((), ())),
            preferred_element_type=jnp.float32,
        )

    own = product_of(w1_ref)
    other = product_of(w2_ref)

    def emit(product, offset):
        for g in range(act_ref.shape[1] // shard):
            cols = pl.ds(pl.multiple_of(g * shard + offset, HALF), HALF)
            normed = act_ref[:, cols].astype(jnp.float32) / rms_ref[...]
            part = product[:, g * HALF : (g + 1) * HALF].reshape(groups, tokens, HALF)
            out_ref[g, :, pl.ds(pl.multiple_of(offset, HALF), HALF)] = jnp.sum(
                part * normed[None], axis=1
            )

    core = core_ref[0]
    emit(own, core * HALF)
    emit(other, (1 - core) * HALF)


def backward_terms(core, back_rows, first, second, activations, rms, groups):
    tokens, width = activations.shape
    keys = first.shape[2]
    tile = 2 * BWD_TILE
    shards = tile // (2 * HALF)
    return pl.pallas_call(
        backward_kernel,
        grid_spec=pltpu.PrefetchScalarGridSpec(
            num_scalar_prefetch=1,
            grid=(width // tile,),
            in_specs=[
                pl.BlockSpec((groups * tokens, keys), lambda k, c: (0, 0)),
                pl.BlockSpec((shards, HALF, keys), lambda k, c: (k, 0, 0)),
                pl.BlockSpec((shards, HALF, keys), lambda k, c: (k, 0, 0)),
                pl.BlockSpec((tokens, tile), lambda k, c: (0, k)),
                pl.BlockSpec((tokens, HALF), lambda k, c: (0, 0)),
            ],
            out_specs=pl.BlockSpec((shards, groups, 2 * HALF), lambda k, c: (k, 0, 0)),
        ),
        out_shape=jax.ShapeDtypeStruct((width // (2 * HALF), groups, 2 * HALF), jnp.float32),
        compiler_params=pltpu.CompilerParams(dimension_semantics=("arbitrary",)),
    )(core, back_rows, first, second, activations, rms)


def per_device(activations, gain, key_weight, key_gain, cotangent, directions):
    tokens_dev = activations.shape[0]
    total_tokens = tokens_dev * lax.axis_size("dp") * lax.axis_size("fsdp")
    values = activations.astype(jnp.float32)
    rms = jnp.sqrt(jnp.mean(values * values, axis=1, keepdims=True) + 1e-05)
    rms = jnp.broadcast_to(rms, (tokens_dev, HALF))
    groups = directions.shape[1] + 1
    core = (lax.axis_index("dp") % 2).astype(jnp.int32).reshape(1)

    first, second = gather_weight(key_weight, gain, directions)
    kg_row = key_gain[None, :]

    back_rows = forward_rows(core, activations, rms, first, second, cotangent, kg_row)
    partial_terms = backward_terms(core, back_rows, first, second, activations, rms, groups)
    shared_rows = jnp.sum(lax.all_to_all(partial_terms, "fsdp", 0, 0, tiled=True), axis=0)
    summed = sum_over_pairs(shared_rows, "dp") / math.sqrt(total_tokens)
    images = summed[1:]
    gram_matrix = of_everyone(
        jnp.dot(images, images.T, precision=lax.Precision.HIGHEST), "fsdp"
    )
    factor = jnp.linalg.cholesky(gram_matrix)
    ortho_basis = math.sqrt(D) * jax.scipy.linalg.solve_triangular(factor, images, lower=True)
    return (ortho_basis.T, summed[0])


def solution(mesh):
    placed = (
        P(("dp", "fsdp"), None),
        P("fsdp"),
        P("fsdp", None),
        P(),
        P(("dp", "fsdp"), None),
        P("fsdp", None),
    )
    return jax.shard_map(
        per_device,
        mesh=mesh,
        in_specs=placed,
        out_specs=(P("fsdp", None), P("fsdp")),
        check_vma=False,
    )
```

```python
import math

import jax
import jax.numpy as jnp
from jax import lax
from jax.experimental import pallas as pl
from jax.experimental.pallas import tpu as pltpu
from jax.sharding import PartitionSpec as P

D = 8192
HEADS_KV = 4
HEAD_DIM = 128
HALF = 128
EXTRA_ROWS = 8
GROUPS = 9
FWD_TILE = 1024
BWD_TILE = 512


def in_blocks(shard, dim, devices):
    shape = shard.shape
    parts = shard.reshape(*shape[:dim], devices, shape[dim] // devices, *shape[dim + 1 :])
    return jnp.moveaxis(parts, dim, 0)


def sum_at_owner(shard, axis, dim):
    devices = lax.axis_size(axis)
    parts = lax.all_to_all(in_blocks(shard, dim, devices), axis, 0, 0, tiled=True)
    return jnp.sum(parts, axis=0)


def copy_for_each(shard, axis):
    copies = jnp.broadcast_to(shard, (lax.axis_size(axis), *shard.shape))
    return lax.all_to_all(copies, axis, split_axis=0, concat_axis=0, tiled=True)


def of_everyone(shard, axis):
    return copy_for_each(shard, axis).sum(axis=0)


def sum_over_pairs(shard, axis):
    devices = lax.axis_size(axis)
    step = 1
    while step < devices:
        shard = shard + lax.ppermute(shard, axis, [(i, i ^ step) for i in range(devices)])
        step *= 2
    return shard


def gather_weight(key_weight, gain, directions):
    rows, width = key_weight.shape
    half = rows // 2
    core = lax.axis_index("dp") % 2
    mine = lax.dynamic_slice_in_dim(key_weight, core * half, half, 0)
    extra = jnp.concatenate([gain[None, :], directions.T], axis=0)
    count = extra.shape[0]
    per_row = width // rows
    packed_rows = -(-count // per_row)
    extra = jnp.pad(extra, ((0, packed_rows * per_row - count), (0, 0)))
    extra = extra.reshape(packed_rows, width)
    extra = jnp.pad(extra, ((0, EXTRA_ROWS - packed_rows), (0, 0)))
    piece = jnp.concatenate([mine, extra], axis=0)
    first = copy_for_each(piece, "fsdp")
    dp = lax.axis_size("dp")
    second = lax.ppermute(first, "dp", [(i, i ^ 1) for i in range(dp)])
    return first, second


def middle_rows(acc, cot, key_gain_row, back_ref):
    tokens = cot.shape[0]
    groups = acc.shape[0] // tokens
    for h in range(HEADS_KV):
        cols = slice(h * HEAD_DIM, (h + 1) * HEAD_DIM)
        key = acc[0:tokens, cols]
        weighted = cot[:, cols].astype(jnp.float32) * key_gain_row
        key_scale = jnp.sqrt(jnp.sum(key * key, axis=-1, keepdims=True) / HEAD_DIM + 1e-05)
        unit_keys = key / key_scale
        inner_sum = jnp.sum(unit_keys * weighted, axis=-1, keepdims=True)
        grad_keys = (weighted - unit_keys * inner_sum / HEAD_DIM) / key_scale
        back_ref[0:tokens, cols] = grad_keys.astype(back_ref.dtype)
        for j in range(1, groups):
            tangent = acc[j * tokens : (j + 1) * tokens, cols]
            shift_rate = jnp.sum(unit_keys * tangent, axis=-1, keepdims=True) / HEAD_DIM
            unit_change = (tangent - unit_keys * shift_rate) / key_scale
            along = jnp.sum(unit_change * weighted, axis=-1, keepdims=True)
            second = -(unit_change * inner_sum + unit_keys * along) / (
                HEAD_DIM * key_scale
            ) - grad_keys * shift_rate / key_scale
            back_ref[j * tokens : (j + 1) * tokens, cols] = second.astype(back_ref.dtype)


def build_lhs(act_ref, rms_ref, ext_ref, lhs_ref, offset):
    tokens = act_ref.shape[0]
    shard = 2 * HALF
    per_row = ext_ref.shape[2] // shard
    for g in range(act_ref.shape[1] // shard):
        cols = pl.ds(pl.multiple_of(g * shard + offset, HALF), HALF)
        normed = act_ref[:, cols].astype(jnp.float32) / rms_ref[...]
        for j in range(GROUPS):
            lanes = pl.ds(pl.multiple_of((j % per_row) * shard + offset, HALF), HALF)
            scale = ext_ref[g, pl.ds(j // per_row, 1), lanes].astype(jnp.float32)
            lhs_ref[j * tokens : (j + 1) * tokens, g * HALF : (g + 1) * HALF] = (
                normed * scale
            ).astype(jnp.bfloat16)


def build_for(core_ref, act_ref, rms_ref, ext_ref, lhs_ref, own):
    core = core_ref[0] if own else 1 - core_ref[0]
    build_lhs(act_ref, rms_ref, ext_ref, lhs_ref, core * HALF)


def weight_tile(w_ref):
    shards, rows, width = w_ref.shape
    return w_ref[...].reshape(shards * rows, width)


def forward_first_kernel(core_ref, act_ref, rms_ref, gd_ref, w_ref, out_ref, lhs_ref):
    k = pl.program_id(0)

    @pl.when(k == 0)
    def _():
        out_ref[...] = jnp.zeros_like(out_ref)

    build_for(core_ref, act_ref, rms_ref, gd_ref, lhs_ref, True)
    out_ref[...] += jnp.dot(lhs_ref[...], weight_tile(w_ref), preferred_element_type=jnp.float32)


def forward_second_kernel(
    core_ref, act_ref, rms_ref, gd_ref, w_ref, acc_in_ref, cot_ref, kg_ref, back_ref, lhs_ref, acc_ref
):
    k = pl.program_id(0)

    @pl.when(k == 0)
    def _():
        acc_ref[...] = acc_in_ref[...]

    build_for(core_ref, act_ref, rms_ref, gd_ref, lhs_ref, False)
    acc_ref[...] += jnp.dot(lhs_ref[...], weight_tile(w_ref), preferred_element_type=jnp.float32)

    @pl.when(k == pl.num_programs(0) - 1)
    def _():
        middle_rows(acc_ref[...], cot_ref[...], kg_ref[...], back_ref)


def forward_rows(core, activations, rms, first, second, cot, kg_row):
    tokens, width = activations.shape
    groups = GROUPS
    keys = first.shape[2]
    tile = 2 * FWD_TILE
    shards = tile // (2 * HALF)
    common = [
        pl.BlockSpec((tokens, tile), lambda k, c: (0, k)),
        pl.BlockSpec((tokens, HALF), lambda k, c: (0, 0)),
        pl.BlockSpec((shards, EXTRA_ROWS, keys), lambda k, c: (k, HALF // EXTRA_ROWS, 0)),
        pl.BlockSpec((shards, HALF, keys), lambda k, c: (k, 0, 0)),
    ]
    params = pltpu.CompilerParams(dimension_semantics=("arbitrary",))
    acc = pl.pallas_call(
        forward_first_kernel,
        grid_spec=pltpu.PrefetchScalarGridSpec(
            num_scalar_prefetch=1,
            grid=(width // tile,),
            in_specs=common,
            out_specs=pl.BlockSpec((groups * tokens, keys), lambda k, c: (0, 0)),
            scratch_shapes=[pltpu.VMEM((groups * tokens, FWD_TILE), jnp.bfloat16)],
        ),
        out_shape=jax.ShapeDtypeStruct((groups * tokens, keys), jnp.float32),
        compiler_params=params,
    )(core, activations, rms, first, first)
    return pl.pallas_call(
        forward_second_kernel,
        grid_spec=pltpu.PrefetchScalarGridSpec(
            num_scalar_prefetch=1,
            grid=(width // tile,),
            in_specs=common
            + [
                pl.BlockSpec((groups * tokens, keys), lambda k, c: (0, 0)),
                pl.BlockSpec((tokens, keys), lambda k, c: (0, 0)),
                pl.BlockSpec((1, HEAD_DIM), lambda k, c: (0, 0)),
            ],
            out_specs=pl.BlockSpec((groups * tokens, keys), lambda k, c: (0, 0)),
            scratch_shapes=[
                pltpu.VMEM((groups * tokens, FWD_TILE), jnp.bfloat16),
                pltpu.VMEM((groups * tokens, keys), jnp.float32),
            ],
        ),
        out_shape=jax.ShapeDtypeStruct((groups * tokens, keys), jnp.bfloat16),
        compiler_params=params,
    )(core, activations, rms, first, second, acc, cot, kg_row)


def backward_kernel(core_ref, back_ref, w1_ref, w2_ref, act_ref, rms_ref, out_ref):
    tokens = act_ref.shape[0]
    groups = out_ref.shape[1]
    shard = 2 * HALF

    def product_of(w_ref):
        return lax.dot_general(
            back_ref[...],
            weight_tile(w_ref),
            (((1,), (1,)), ((), ())),
            preferred_element_type=jnp.float32,
        )

    own = product_of(w1_ref)
    other = product_of(w2_ref)

    def emit(product, offset):
        for g in range(act_ref.shape[1] // shard):
            cols = pl.ds(pl.multiple_of(g * shard + offset, HALF), HALF)
            normed = act_ref[:, cols].astype(jnp.float32) / rms_ref[...]
            part = product[:, g * HALF : (g + 1) * HALF].reshape(groups, tokens, HALF)
            out_ref[g, :, pl.ds(pl.multiple_of(offset, HALF), HALF)] = jnp.sum(
                part * normed[None], axis=1
            )

    core = core_ref[0]
    emit(own, core * HALF)
    emit(other, (1 - core) * HALF)


def backward_terms(core, back_rows, first, second, activations, rms, groups):
    tokens, width = activations.shape
    keys = first.shape[2]
    tile = 2 * BWD_TILE
    shards = tile // (2 * HALF)
    return pl.pallas_call(
        backward_kernel,
        grid_spec=pltpu.PrefetchScalarGridSpec(
            num_scalar_prefetch=1,
            grid=(width // tile,),
            in_specs=[
                pl.BlockSpec((groups * tokens, keys), lambda k, c: (0, 0)),
                pl.BlockSpec((shards, HALF, keys), lambda k, c: (k, 0, 0)),
                pl.BlockSpec((shards, HALF, keys), lambda k, c: (k, 0, 0)),
                pl.BlockSpec((tokens, tile), lambda k, c: (0, k)),
                pl.BlockSpec((tokens, HALF), lambda k, c: (0, 0)),
            ],
            out_specs=pl.BlockSpec((shards, groups, 2 * HALF), lambda k, c: (k, 0, 0)),
        ),
        out_shape=jax.ShapeDtypeStruct((width // (2 * HALF), groups, 2 * HALF), jnp.float32),
        compiler_params=pltpu.CompilerParams(dimension_semantics=("arbitrary",)),
    )(core, back_rows, first, second, activations, rms)


def per_device(activations, gain, key_weight, key_gain, cotangent, directions):
    tokens_dev = activations.shape[0]
    total_tokens = tokens_dev * lax.axis_size("dp") * lax.axis_size("fsdp")
    values = activations.astype(jnp.float32)
    rms = jnp.sqrt(jnp.mean(values * values, axis=1, keepdims=True) + 1e-05)
    rms = jnp.broadcast_to(rms, (tokens_dev, HALF))
    groups = directions.shape[1] + 1
    core = (lax.axis_index("dp") % 2).astype(jnp.int32).reshape(1)

    first, second = gather_weight(key_weight, gain, directions)
    kg_row = key_gain[None, :]

    back_rows = forward_rows(core, activations, rms, first, second, cotangent, kg_row)
    partial_terms = backward_terms(core, back_rows, first, second, activations, rms, groups)
    shared_rows = jnp.sum(lax.all_to_all(partial_terms, "fsdp", 0, 0, tiled=True), axis=0)
    summed = sum_over_pairs(shared_rows, "dp") / math.sqrt(total_tokens)
    images = summed[1:]
    gram_matrix = of_everyone(
        jnp.dot(images, images.T, precision=lax.Precision.HIGHEST), "fsdp"
    )
    factor = jnp.linalg.cholesky(gram_matrix)
    ortho_basis = math.sqrt(D) * jax.scipy.linalg.solve_triangular(factor, images, lower=True)
    return (ortho_basis.T, summed[0])


def solution(mesh):
    placed = (
        P(("dp", "fsdp"), None),
        P("fsdp"),
        P("fsdp", None),
        P(),
        P(("dp", "fsdp"), None),
        P("fsdp", None),
    )
    return jax.shard_map(
        per_device,
        mesh=mesh,
        in_specs=placed,
        out_specs=(P("fsdp", None), P("fsdp")),
        check_vma=False,
    )
```

```python
import math

import jax
import jax.numpy as jnp
from jax import lax
from jax.experimental import pallas as pl
from jax.experimental.pallas import tpu as pltpu
from jax.sharding import PartitionSpec as P

D = 8192
HEADS_KV = 4
HEAD_DIM = 128
HALF = 128
EXTRA_ROWS = 8
GROUPS = 9
FWD_TILE = 2048
BWD_TILE = 1024


def in_blocks(shard, dim, devices):
    shape = shard.shape
    parts = shard.reshape(*shape[:dim], devices, shape[dim] // devices, *shape[dim + 1 :])
    return jnp.moveaxis(parts, dim, 0)


def sum_at_owner(shard, axis, dim):
    devices = lax.axis_size(axis)
    parts = lax.all_to_all(in_blocks(shard, dim, devices), axis, 0, 0, tiled=True)
    return jnp.sum(parts, axis=0)


def copy_for_each(shard, axis):
    copies = jnp.broadcast_to(shard, (lax.axis_size(axis), *shard.shape))
    return lax.all_to_all(copies, axis, split_axis=0, concat_axis=0, tiled=True)


def of_everyone(shard, axis):
    return copy_for_each(shard, axis).sum(axis=0)


def sum_over_pairs(shard, axis):
    devices = lax.axis_size(axis)
    step = 1
    while step < devices:
        shard = shard + lax.ppermute(shard, axis, [(i, i ^ step) for i in range(devices)])
        step *= 2
    return shard


def gather_weight(key_weight, gain, directions):
    rows, width = key_weight.shape
    half = rows // 2
    core = lax.axis_index("dp") % 2
    mine = lax.dynamic_slice_in_dim(key_weight, core * half, half, 0)
    extra = jnp.concatenate([gain[None, :], directions.T], axis=0)
    count = extra.shape[0]
    per_row = width // rows
    packed_rows = -(-count // per_row)
    extra = jnp.pad(extra, ((0, packed_rows * per_row - count), (0, 0)))
    extra = extra.reshape(packed_rows, width)
    extra = jnp.pad(extra, ((0, EXTRA_ROWS - packed_rows), (0, 0)))
    piece = jnp.concatenate([mine, extra], axis=0)
    first = copy_for_each(piece, "fsdp")
    dp = lax.axis_size("dp")
    second = lax.ppermute(first, "dp", [(i, i ^ 1) for i in range(dp)])
    return first, second


def middle_rows(acc, cot, key_gain_row, back_ref):
    tokens = cot.shape[0]
    groups = acc.shape[0] // tokens
    for h in range(HEADS_KV):
        cols = slice(h * HEAD_DIM, (h + 1) * HEAD_DIM)
        key = acc[0:tokens, cols]
        weighted = cot[:, cols].astype(jnp.float32) * key_gain_row
        key_scale = jnp.sqrt(jnp.sum(key * key, axis=-1, keepdims=True) / HEAD_DIM + 1e-05)
        unit_keys = key / key_scale
        inner_sum = jnp.sum(unit_keys * weighted, axis=-1, keepdims=True)
        grad_keys = (weighted - unit_keys * inner_sum / HEAD_DIM) / key_scale
        back_ref[0:tokens, cols] = grad_keys.astype(back_ref.dtype)
        for j in range(1, groups):
            tangent = acc[j * tokens : (j + 1) * tokens, cols]
            shift_rate = jnp.sum(unit_keys * tangent, axis=-1, keepdims=True) / HEAD_DIM
            unit_change = (tangent - unit_keys * shift_rate) / key_scale
            along = jnp.sum(unit_change * weighted, axis=-1, keepdims=True)
            second = -(unit_change * inner_sum + unit_keys * along) / (
                HEAD_DIM * key_scale
            ) - grad_keys * shift_rate / key_scale
            back_ref[j * tokens : (j + 1) * tokens, cols] = second.astype(back_ref.dtype)


def build_lhs(act_ref, rms_ref, ext_ref, lhs_ref, offset):
    tokens = act_ref.shape[0]
    shard = 2 * HALF
    per_row = ext_ref.shape[2] // shard
    for g in range(act_ref.shape[1] // shard):
        cols = pl.ds(pl.multiple_of(g * shard + offset, HALF), HALF)
        normed = act_ref[:, cols].astype(jnp.float32) / rms_ref[...]
        for j in range(GROUPS):
            lanes = pl.ds(pl.multiple_of((j % per_row) * shard + offset, HALF), HALF)
            scale = ext_ref[g, pl.ds(j // per_row, 1), lanes].astype(jnp.float32)
            lhs_ref[j * tokens : (j + 1) * tokens, g * HALF : (g + 1) * HALF] = (
                normed * scale
            ).astype(jnp.bfloat16)


def build_for(core_ref, act_ref, rms_ref, ext_ref, lhs_ref, own):
    core = core_ref[0] if own else 1 - core_ref[0]
    build_lhs(act_ref, rms_ref, ext_ref, lhs_ref, core * HALF)


def weight_tile(w_ref):
    shards, rows, width = w_ref.shape
    return w_ref[...].reshape(shards * rows, width)


def forward_first_kernel(core_ref, act_ref, rms_ref, gd_ref, w_ref, out_ref, lhs_ref):
    k = pl.program_id(0)

    @pl.when(k == 0)
    def _():
        out_ref[...] = jnp.zeros_like(out_ref)

    build_for(core_ref, act_ref, rms_ref, gd_ref, lhs_ref, True)
    out_ref[...] += jnp.dot(lhs_ref[...], weight_tile(w_ref), preferred_element_type=jnp.float32)


def forward_second_kernel(
    core_ref, act_ref, rms_ref, gd_ref, w_ref, acc_in_ref, cot_ref, kg_ref, back_ref, lhs_ref, acc_ref
):
    k = pl.program_id(0)

    @pl.when(k == 0)
    def _():
        acc_ref[...] = acc_in_ref[...]

    build_for(core_ref, act_ref, rms_ref, gd_ref, lhs_ref, False)
    acc_ref[...] += jnp.dot(lhs_ref[...], weight_tile(w_ref), preferred_element_type=jnp.float32)

    @pl.when(k == pl.num_programs(0) - 1)
    def _():
        middle_rows(acc_ref[...], cot_ref[...], kg_ref[...], back_ref)


def forward_rows(core, activations, rms, first, second, cot, kg_row):
    tokens, width = activations.shape
    groups = GROUPS
    keys = first.shape[2]
    tile = 2 * FWD_TILE
    shards = tile // (2 * HALF)
    common = [
        pl.BlockSpec((tokens, tile), lambda k, c: (0, k)),
        pl.BlockSpec((tokens, HALF), lambda k, c: (0, 0)),
        pl.BlockSpec((shards, EXTRA_ROWS, keys), lambda k, c: (k, HALF // EXTRA_ROWS, 0)),
        pl.BlockSpec((shards, HALF, keys), lambda k, c: (k, 0, 0)),
    ]
    params = pltpu.CompilerParams(dimension_semantics=("arbitrary",))
    acc = pl.pallas_call(
        forward_first_kernel,
        grid_spec=pltpu.PrefetchScalarGridSpec(
            num_scalar_prefetch=1,
            grid=(width // tile,),
            in_specs=common,
            out_specs=pl.BlockSpec((groups * tokens, keys), lambda k, c: (0, 0)),
            scratch_shapes=[pltpu.VMEM((groups * tokens, FWD_TILE), jnp.bfloat16)],
        ),
        out_shape=jax.ShapeDtypeStruct((groups * tokens, keys), jnp.float32),
        compiler_params=params,
    )(core, activations, rms, first, first)
    return pl.pallas_call(
        forward_second_kernel,
        grid_spec=pltpu.PrefetchScalarGridSpec(
            num_scalar_prefetch=1,
            grid=(width // tile,),
            in_specs=common
            + [
                pl.BlockSpec((groups * tokens, keys), lambda k, c: (0, 0)),
                pl.BlockSpec((tokens, keys), lambda k, c: (0, 0)),
                pl.BlockSpec((1, HEAD_DIM), lambda k, c: (0, 0)),
            ],
            out_specs=pl.BlockSpec((groups * tokens, keys), lambda k, c: (0, 0)),
            scratch_shapes=[
                pltpu.VMEM((groups * tokens, FWD_TILE), jnp.bfloat16),
                pltpu.VMEM((groups * tokens, keys), jnp.float32),
            ],
        ),
        out_shape=jax.ShapeDtypeStruct((groups * tokens, keys), jnp.bfloat16),
        compiler_params=params,
    )(core, activations, rms, first, second, acc, cot, kg_row)


def backward_kernel(core_ref, back_ref, w1_ref, w2_ref, act_ref, rms_ref, out_ref):
    tokens = act_ref.shape[0]
    groups = out_ref.shape[1]
    shard = 2 * HALF

    def product_of(w_ref):
        return lax.dot_general(
            back_ref[...],
            weight_tile(w_ref),
            (((1,), (1,)), ((), ())),
            preferred_element_type=jnp.float32,
        )

    own = product_of(w1_ref)
    other = product_of(w2_ref)

    def emit(product, offset):
        for g in range(act_ref.shape[1] // shard):
            cols = pl.ds(pl.multiple_of(g * shard + offset, HALF), HALF)
            normed = act_ref[:, cols].astype(jnp.float32) / rms_ref[...]
            part = product[:, g * HALF : (g + 1) * HALF].reshape(groups, tokens, HALF)
            out_ref[g, :, pl.ds(pl.multiple_of(offset, HALF), HALF)] = jnp.sum(
                part * normed[None], axis=1
            )

    core = core_ref[0]
    emit(own, core * HALF)
    emit(other, (1 - core) * HALF)


def backward_terms(core, back_rows, first, second, activations, rms, groups):
    tokens, width = activations.shape
    keys = first.shape[2]
    tile = 2 * BWD_TILE
    shards = tile // (2 * HALF)
    return pl.pallas_call(
        backward_kernel,
        grid_spec=pltpu.PrefetchScalarGridSpec(
            num_scalar_prefetch=1,
            grid=(width // tile,),
            in_specs=[
                pl.BlockSpec((groups * tokens, keys), lambda k, c: (0, 0)),
                pl.BlockSpec((shards, HALF, keys), lambda k, c: (k, 0, 0)),
                pl.BlockSpec((shards, HALF, keys), lambda k, c: (k, 0, 0)),
                pl.BlockSpec((tokens, tile), lambda k, c: (0, k)),
                pl.BlockSpec((tokens, HALF), lambda k, c: (0, 0)),
            ],
            out_specs=pl.BlockSpec((shards, groups, 2 * HALF), lambda k, c: (k, 0, 0)),
        ),
        out_shape=jax.ShapeDtypeStruct((width // (2 * HALF), groups, 2 * HALF), jnp.float32),
        compiler_params=pltpu.CompilerParams(dimension_semantics=("arbitrary",)),
    )(core, back_rows, first, second, activations, rms)


def per_device(activations, gain, key_weight, key_gain, cotangent, directions):
    tokens_dev = activations.shape[0]
    total_tokens = tokens_dev * lax.axis_size("dp") * lax.axis_size("fsdp")
    values = activations.astype(jnp.float32)
    rms = jnp.sqrt(jnp.mean(values * values, axis=1, keepdims=True) + 1e-05)
    rms = jnp.broadcast_to(rms, (tokens_dev, HALF))
    groups = directions.shape[1] + 1
    core = (lax.axis_index("dp") % 2).astype(jnp.int32).reshape(1)

    first, second = gather_weight(key_weight, gain, directions)
    kg_row = key_gain[None, :]

    back_rows = forward_rows(core, activations, rms, first, second, cotangent, kg_row)
    partial_terms = backward_terms(core, back_rows, first, second, activations, rms, groups)
    shared_rows = jnp.sum(lax.all_to_all(partial_terms, "fsdp", 0, 0, tiled=True), axis=0)
    summed = sum_over_pairs(shared_rows, "dp") / math.sqrt(total_tokens)
    images = summed[1:]
    gram_matrix = of_everyone(
        jnp.dot(images, images.T, precision=lax.Precision.HIGHEST), "fsdp"
    )
    factor = jnp.linalg.cholesky(gram_matrix)
    ortho_basis = math.sqrt(D) * jax.scipy.linalg.solve_triangular(factor, images, lower=True)
    return (ortho_basis.T, summed[0])


def solution(mesh):
    placed = (
        P(("dp", "fsdp"), None),
        P("fsdp"),
        P("fsdp", None),
        P(),
        P(("dp", "fsdp"), None),
        P("fsdp", None),
    )
    return jax.shard_map(
        per_device,
        mesh=mesh,
        in_specs=placed,
        out_specs=(P("fsdp", None), P("fsdp")),
        check_vma=False,
    )
```

```python
import math

import jax
import jax.numpy as jnp
from jax import lax
from jax.experimental import pallas as pl
from jax.experimental.pallas import tpu as pltpu
from jax.sharding import PartitionSpec as P

D = 8192
HEADS_KV = 4
HEAD_DIM = 128
HALF = 128
EXTRA_ROWS = 8
GROUPS = 9
FWD_TILE = 1024
BWD_TILE = 1024


def in_blocks(shard, dim, devices):
    shape = shard.shape
    parts = shard.reshape(*shape[:dim], devices, shape[dim] // devices, *shape[dim + 1 :])
    return jnp.moveaxis(parts, dim, 0)


def sum_at_owner(shard, axis, dim):
    devices = lax.axis_size(axis)
    parts = lax.all_to_all(in_blocks(shard, dim, devices), axis, 0, 0, tiled=True)
    return jnp.sum(parts, axis=0)


def copy_for_each(shard, axis):
    copies = jnp.broadcast_to(shard, (lax.axis_size(axis), *shard.shape))
    return lax.all_to_all(copies, axis, split_axis=0, concat_axis=0, tiled=True)


def of_everyone(shard, axis):
    return copy_for_each(shard, axis).sum(axis=0)


def sum_over_pairs(shard, axis):
    devices = lax.axis_size(axis)
    step = 1
    while step < devices:
        shard = shard + lax.ppermute(shard, axis, [(i, i ^ step) for i in range(devices)])
        step *= 2
    return shard


def gather_weight(key_weight, gain, directions):
    rows, width = key_weight.shape
    half = rows // 2
    core = lax.axis_index("dp") % 2
    mine = lax.dynamic_slice_in_dim(key_weight, core * half, half, 0)
    extra = jnp.concatenate([gain[None, :], directions.T], axis=0)
    count = extra.shape[0]
    per_row = width // rows
    packed_rows = -(-count // per_row)
    extra = jnp.pad(extra, ((0, packed_rows * per_row - count), (0, 0)))
    extra = extra.reshape(packed_rows, width)
    extra = jnp.pad(extra, ((0, EXTRA_ROWS - packed_rows), (0, 0)))
    piece = jnp.concatenate([mine, extra], axis=0)
    first = copy_for_each(piece, "fsdp")
    dp = lax.axis_size("dp")
    second = lax.ppermute(first, "dp", [(i, i ^ 1) for i in range(dp)])
    return first, second


def middle_rows(acc, cot, key_gain_row, back_ref):
    tokens = cot.shape[0]
    groups = acc.shape[0] // tokens
    for h in range(HEADS_KV):
        cols = slice(h * HEAD_DIM, (h + 1) * HEAD_DIM)
        key = acc[0:tokens, cols]
        weighted = cot[:, cols].astype(jnp.float32) * key_gain_row
        key_scale = jnp.sqrt(jnp.sum(key * key, axis=-1, keepdims=True) / HEAD_DIM + 1e-05)
        unit_keys = key / key_scale
        inner_sum = jnp.sum(unit_keys * weighted, axis=-1, keepdims=True)
        grad_keys = (weighted - unit_keys * inner_sum / HEAD_DIM) / key_scale
        back_ref[0:tokens, cols] = grad_keys.astype(back_ref.dtype)
        for j in range(1, groups):
            tangent = acc[j * tokens : (j + 1) * tokens, cols]
            shift_rate = jnp.sum(unit_keys * tangent, axis=-1, keepdims=True) / HEAD_DIM
            unit_change = (tangent - unit_keys * shift_rate) / key_scale
            along = jnp.sum(unit_change * weighted, axis=-1, keepdims=True)
            second = -(unit_change * inner_sum + unit_keys * along) / (
                HEAD_DIM * key_scale
            ) - grad_keys * shift_rate / key_scale
            back_ref[j * tokens : (j + 1) * tokens, cols] = second.astype(back_ref.dtype)


def build_lhs(act_ref, rms_ref, ext_ref, lhs_ref, offset):
    tokens = act_ref.shape[0]
    shard = 2 * HALF
    per_row = ext_ref.shape[2] // shard
    for g in range(act_ref.shape[1] // shard):
        cols = pl.ds(pl.multiple_of(g * shard + offset, HALF), HALF)
        normed = act_ref[:, cols].astype(jnp.float32) / rms_ref[...]
        for j in range(GROUPS):
            lanes = pl.ds(pl.multiple_of((j % per_row) * shard + offset, HALF), HALF)
            scale = ext_ref[g, pl.ds(j // per_row, 1), lanes].astype(jnp.float32)
            lhs_ref[j * tokens : (j + 1) * tokens, g * HALF : (g + 1) * HALF] = (
                normed * scale
            ).astype(jnp.bfloat16)


def build_for(core_ref, act_ref, rms_ref, ext_ref, lhs_ref, own):
    core = core_ref[0] if own else 1 - core_ref[0]
    build_lhs(act_ref, rms_ref, ext_ref, lhs_ref, core * HALF)


def weight_tile(w_ref):
    shards, rows, width = w_ref.shape
    return w_ref[...].reshape(shards * rows, width)


def forward_first_kernel(core_ref, act_ref, rms_ref, gd_ref, w_ref, out_ref, lhs_ref):
    k = pl.program_id(0)

    build_for(core_ref, act_ref, rms_ref, gd_ref, lhs_ref, True)
    part = jnp.dot(lhs_ref[...], weight_tile(w_ref), preferred_element_type=jnp.float32)

    @pl.when(k == 0)
    def _():
        out_ref[...] = part

    @pl.when(k > 0)
    def _():
        out_ref[...] += part


def forward_second_kernel(
    core_ref, act_ref, rms_ref, gd_ref, w_ref, acc_in_ref, cot_ref, kg_ref, back_ref, lhs_ref, acc_ref
):
    k = pl.program_id(0)

    build_for(core_ref, act_ref, rms_ref, gd_ref, lhs_ref, False)
    part = jnp.dot(lhs_ref[...], weight_tile(w_ref), preferred_element_type=jnp.float32)

    @pl.when(k == 0)
    def _():
        acc_ref[...] = acc_in_ref[...] + part

    @pl.when(k > 0)
    def _():
        acc_ref[...] += part

    @pl.when(k == pl.num_programs(0) - 1)
    def _():
        middle_rows(acc_ref[...], cot_ref[...], kg_ref[...], back_ref)


def forward_rows(core, activations, rms, first, second, cot, kg_row):
    tokens, width = activations.shape
    groups = GROUPS
    keys = first.shape[2]
    tile = 2 * FWD_TILE
    shards = tile // (2 * HALF)
    common = [
        pl.BlockSpec((tokens, tile), lambda k, c: (0, k)),
        pl.BlockSpec((tokens, HALF), lambda k, c: (0, 0)),
        pl.BlockSpec((shards, EXTRA_ROWS, keys), lambda k, c: (k, HALF // EXTRA_ROWS, 0)),
        pl.BlockSpec((shards, HALF, keys), lambda k, c: (k, 0, 0)),
    ]
    params = pltpu.CompilerParams(dimension_semantics=("arbitrary",))
    acc = pl.pallas_call(
        forward_first_kernel,
        grid_spec=pltpu.PrefetchScalarGridSpec(
            num_scalar_prefetch=1,
            grid=(width // tile,),
            in_specs=common,
            out_specs=pl.BlockSpec((groups * tokens, keys), lambda k, c: (0, 0)),
            scratch_shapes=[pltpu.VMEM((groups * tokens, FWD_TILE), jnp.bfloat16)],
        ),
        out_shape=jax.ShapeDtypeStruct((groups * tokens, keys), jnp.float32),
        compiler_params=params,
    )(core, activations, rms, first, first)
    return pl.pallas_call(
        forward_second_kernel,
        grid_spec=pltpu.PrefetchScalarGridSpec(
            num_scalar_prefetch=1,
            grid=(width // tile,),
            in_specs=common
            + [
                pl.BlockSpec((groups * tokens, keys), lambda k, c: (0, 0)),
                pl.BlockSpec((tokens, keys), lambda k, c: (0, 0)),
                pl.BlockSpec((1, HEAD_DIM), lambda k, c: (0, 0)),
            ],
            out_specs=pl.BlockSpec((groups * tokens, keys), lambda k, c: (0, 0)),
            scratch_shapes=[
                pltpu.VMEM((groups * tokens, FWD_TILE), jnp.bfloat16),
                pltpu.VMEM((groups * tokens, keys), jnp.float32),
            ],
        ),
        out_shape=jax.ShapeDtypeStruct((groups * tokens, keys), jnp.bfloat16),
        compiler_params=params,
    )(core, activations, rms, first, second, acc, cot, kg_row)


def backward_kernel(core_ref, back_ref, w1_ref, w2_ref, act_ref, rms_ref, out_ref):
    tokens = act_ref.shape[0]
    groups = out_ref.shape[1]
    shard = 2 * HALF

    def product_of(w_ref):
        return lax.dot_general(
            back_ref[...],
            weight_tile(w_ref),
            (((1,), (1,)), ((), ())),
            preferred_element_type=jnp.float32,
        )

    own = product_of(w1_ref)
    other = product_of(w2_ref)

    def emit(product, offset):
        for g in range(act_ref.shape[1] // shard):
            cols = pl.ds(pl.multiple_of(g * shard + offset, HALF), HALF)
            normed = act_ref[:, cols].astype(jnp.float32) / rms_ref[...]
            part = product[:, g * HALF : (g + 1) * HALF].reshape(groups, tokens, HALF)
            out_ref[g, :, pl.ds(pl.multiple_of(offset, HALF), HALF)] = jnp.sum(
                part * normed[None], axis=1
            )

    core = core_ref[0]
    emit(own, core * HALF)
    emit(other, (1 - core) * HALF)


def backward_terms(core, back_rows, first, second, activations, rms, groups):
    tokens, width = activations.shape
    keys = first.shape[2]
    tile = 2 * BWD_TILE
    shards = tile // (2 * HALF)
    return pl.pallas_call(
        backward_kernel,
        grid_spec=pltpu.PrefetchScalarGridSpec(
            num_scalar_prefetch=1,
            grid=(width // tile,),
            in_specs=[
                pl.BlockSpec((groups * tokens, keys), lambda k, c: (0, 0)),
                pl.BlockSpec((shards, HALF, keys), lambda k, c: (k, 0, 0)),
                pl.BlockSpec((shards, HALF, keys), lambda k, c: (k, 0, 0)),
                pl.BlockSpec((tokens, tile), lambda k, c: (0, k)),
                pl.BlockSpec((tokens, HALF), lambda k, c: (0, 0)),
            ],
            out_specs=pl.BlockSpec((shards, groups, 2 * HALF), lambda k, c: (k, 0, 0)),
        ),
        out_shape=jax.ShapeDtypeStruct((width // (2 * HALF), groups, 2 * HALF), jnp.float32),
        compiler_params=pltpu.CompilerParams(dimension_semantics=("arbitrary",)),
    )(core, back_rows, first, second, activations, rms)


def per_device(activations, gain, key_weight, key_gain, cotangent, directions):
    tokens_dev = activations.shape[0]
    total_tokens = tokens_dev * lax.axis_size("dp") * lax.axis_size("fsdp")
    values = activations.astype(jnp.float32)
    rms = jnp.sqrt(jnp.mean(values * values, axis=1, keepdims=True) + 1e-05)
    rms = jnp.broadcast_to(rms, (tokens_dev, HALF))
    groups = directions.shape[1] + 1
    core = (lax.axis_index("dp") % 2).astype(jnp.int32).reshape(1)

    first, second = gather_weight(key_weight, gain, directions)
    kg_row = key_gain[None, :]

    back_rows = forward_rows(core, activations, rms, first, second, cotangent, kg_row)
    partial_terms = backward_terms(core, back_rows, first, second, activations, rms, groups)
    shared_rows = jnp.sum(lax.all_to_all(partial_terms, "fsdp", 0, 0, tiled=True), axis=0)
    summed = sum_over_pairs(shared_rows, "dp") / math.sqrt(total_tokens)
    images = summed[1:]
    gram_matrix = of_everyone(
        jnp.dot(images, images.T, precision=lax.Precision.HIGHEST), "fsdp"
    )
    factor = jnp.linalg.cholesky(gram_matrix)
    ortho_basis = math.sqrt(D) * jax.scipy.linalg.solve_triangular(factor, images, lower=True)
    return (ortho_basis.T, summed[0])


def solution(mesh):
    placed = (
        P(("dp", "fsdp"), None),
        P("fsdp"),
        P("fsdp", None),
        P(),
        P(("dp", "fsdp"), None),
        P("fsdp", None),
    )
    return jax.shard_map(
        per_device,
        mesh=mesh,
        in_specs=placed,
        out_specs=(P("fsdp", None), P("fsdp")),
        check_vma=False,
    )
```

```python
import math

import jax
import jax.numpy as jnp
from jax import lax
from jax.experimental import pallas as pl
from jax.experimental.pallas import tpu as pltpu
from jax.sharding import PartitionSpec as P

D = 8192
HEADS_KV = 4
HEAD_DIM = 128
HALF = 128
EXTRA_ROWS = 8
GROUPS = 9
FWD_TILE = 1024
BWD_TILE = 1024


def in_blocks(shard, dim, devices):
    shape = shard.shape
    parts = shard.reshape(*shape[:dim], devices, shape[dim] // devices, *shape[dim + 1 :])
    return jnp.moveaxis(parts, dim, 0)


def sum_at_owner(shard, axis, dim):
    devices = lax.axis_size(axis)
    parts = lax.all_to_all(in_blocks(shard, dim, devices), axis, 0, 0, tiled=True)
    return jnp.sum(parts, axis=0)


def copy_for_each(shard, axis):
    copies = jnp.broadcast_to(shard, (lax.axis_size(axis), *shard.shape))
    return lax.all_to_all(copies, axis, split_axis=0, concat_axis=0, tiled=True)


def of_everyone(shard, axis):
    return copy_for_each(shard, axis).sum(axis=0)


def sum_over_pairs(shard, axis):
    devices = lax.axis_size(axis)
    step = 1
    while step < devices:
        shard = shard + lax.ppermute(shard, axis, [(i, i ^ step) for i in range(devices)])
        step *= 2
    return shard


def gather_weight(key_weight, gain, directions):
    rows, width = key_weight.shape
    half = rows // 2
    core = lax.axis_index("dp") % 2
    mine = lax.dynamic_slice_in_dim(key_weight, core * half, half, 0)
    extra = jnp.concatenate([gain[None, :], directions.T], axis=0)
    count = extra.shape[0]
    per_row = width // rows
    packed_rows = -(-count // per_row)
    extra = jnp.pad(extra, ((0, packed_rows * per_row - count), (0, 0)))
    extra = extra.reshape(packed_rows, width)
    extra = jnp.pad(extra, ((0, EXTRA_ROWS - packed_rows), (0, 0)))
    piece = jnp.concatenate([mine, extra], axis=0)
    first = copy_for_each(piece, "fsdp")
    dp = lax.axis_size("dp")
    second = lax.ppermute(first, "dp", [(i, i ^ 1) for i in range(dp)])
    return first, second


def middle_rows(acc, cot, key_gain_row, back_ref):
    tokens = cot.shape[0]
    groups = acc.shape[0] // tokens
    for h in range(HEADS_KV):
        cols = slice(h * HEAD_DIM, (h + 1) * HEAD_DIM)
        key = acc[0:tokens, cols]
        weighted = cot[:, cols].astype(jnp.float32) * key_gain_row
        key_scale = jnp.sqrt(jnp.sum(key * key, axis=-1, keepdims=True) / HEAD_DIM + 1e-05)
        unit_keys = key / key_scale
        inner_sum = jnp.sum(unit_keys * weighted, axis=-1, keepdims=True)
        grad_keys = (weighted - unit_keys * inner_sum / HEAD_DIM) / key_scale
        back_ref[0:tokens, cols] = grad_keys.astype(back_ref.dtype)
        for j in range(1, groups):
            tangent = acc[j * tokens : (j + 1) * tokens, cols]
            shift_rate = jnp.sum(unit_keys * tangent, axis=-1, keepdims=True) / HEAD_DIM
            unit_change = (tangent - unit_keys * shift_rate) / key_scale
            along = jnp.sum(unit_change * weighted, axis=-1, keepdims=True)
            second = -(unit_change * inner_sum + unit_keys * along) / (
                HEAD_DIM * key_scale
            ) - grad_keys * shift_rate / key_scale
            back_ref[j * tokens : (j + 1) * tokens, cols] = second.astype(back_ref.dtype)


def build_lhs(act_ref, rms_ref, ext_ref, lhs_ref, offset):
    tokens = act_ref.shape[0]
    shard = 2 * HALF
    per_row = ext_ref.shape[2] // shard
    for g in range(act_ref.shape[1] // shard):
        cols = pl.ds(pl.multiple_of(g * shard + offset, HALF), HALF)
        normed = act_ref[:, cols].astype(jnp.float32) / rms_ref[...]
        for j in range(GROUPS):
            lanes = pl.ds(pl.multiple_of((j % per_row) * shard + offset, HALF), HALF)
            scale = ext_ref[g, pl.ds(j // per_row, 1), lanes].astype(jnp.float32)
            lhs_ref[j * tokens : (j + 1) * tokens, g * HALF : (g + 1) * HALF] = (
                normed * scale
            ).astype(jnp.bfloat16)


def build_for(core_ref, act_ref, rms_ref, ext_ref, lhs_ref, own):
    core = core_ref[0] if own else 1 - core_ref[0]
    build_lhs(act_ref, rms_ref, ext_ref, lhs_ref, core * HALF)


def weight_tile(w_ref):
    shards, rows, width = w_ref.shape
    return w_ref[...].reshape(shards * rows, width)


def forward_first_kernel(core_ref, act_ref, rms_ref, gd_ref, w_ref, out_ref, lhs_ref):
    k = pl.program_id(0)

    @pl.when(k == 0)
    def _():
        out_ref[...] = jnp.zeros_like(out_ref)

    build_for(core_ref, act_ref, rms_ref, gd_ref, lhs_ref, True)
    out_ref[...] += jnp.dot(lhs_ref[...], weight_tile(w_ref), preferred_element_type=jnp.float32)


def forward_second_kernel(
    core_ref, act_ref, rms_ref, gd_ref, w_ref, acc_in_ref, cot_ref, kg_ref, back_ref, lhs_ref, acc_ref
):
    k = pl.program_id(0)

    @pl.when(k == 0)
    def _():
        acc_ref[...] = acc_in_ref[...]

    build_for(core_ref, act_ref, rms_ref, gd_ref, lhs_ref, False)
    acc_ref[...] += jnp.dot(lhs_ref[...], weight_tile(w_ref), preferred_element_type=jnp.float32)

    @pl.when(k == pl.num_programs(0) - 1)
    def _():
        middle_rows(acc_ref[...], cot_ref[...], kg_ref[...], back_ref)


def forward_rows(core, activations, rms, first, second, cot, kg_row):
    tokens, width = activations.shape
    groups = GROUPS
    keys = first.shape[2]
    tile = 2 * FWD_TILE
    shards = tile // (2 * HALF)
    common = [
        pl.BlockSpec((tokens, tile), lambda k, c: (0, k)),
        pl.BlockSpec((tokens, HALF), lambda k, c: (0, 0)),
        pl.BlockSpec((shards, EXTRA_ROWS, keys), lambda k, c: (k, HALF // EXTRA_ROWS, 0)),
        pl.BlockSpec((shards, HALF, keys), lambda k, c: (k, 0, 0)),
    ]
    params = pltpu.CompilerParams(dimension_semantics=("arbitrary",))
    acc = pl.pallas_call(
        forward_first_kernel,
        grid_spec=pltpu.PrefetchScalarGridSpec(
            num_scalar_prefetch=1,
            grid=(width // tile,),
            in_specs=common,
            out_specs=pl.BlockSpec((groups * tokens, keys), lambda k, c: (0, 0)),
            scratch_shapes=[pltpu.VMEM((groups * tokens, FWD_TILE), jnp.bfloat16)],
        ),
        out_shape=jax.ShapeDtypeStruct((groups * tokens, keys), jnp.float32),
        compiler_params=params,
    )(core, activations, rms, first, first)
    return pl.pallas_call(
        forward_second_kernel,
        grid_spec=pltpu.PrefetchScalarGridSpec(
            num_scalar_prefetch=1,
            grid=(width // tile,),
            in_specs=common
            + [
                pl.BlockSpec((groups * tokens, keys), lambda k, c: (0, 0)),
                pl.BlockSpec((tokens, keys), lambda k, c: (0, 0)),
                pl.BlockSpec((1, HEAD_DIM), lambda k, c: (0, 0)),
            ],
            out_specs=pl.BlockSpec((groups * tokens, keys), lambda k, c: (0, 0)),
            scratch_shapes=[
                pltpu.VMEM((groups * tokens, FWD_TILE), jnp.bfloat16),
                pltpu.VMEM((groups * tokens, keys), jnp.float32),
            ],
        ),
        out_shape=jax.ShapeDtypeStruct((groups * tokens, keys), jnp.bfloat16),
        compiler_params=params,
    )(core, activations, rms, first, second, acc, cot, kg_row)


def backward_kernel(core_ref, back_ref, w1_ref, w2_ref, act_ref, rms_ref, out_ref):
    tokens = act_ref.shape[0]
    groups = out_ref.shape[1]
    shard = 2 * HALF

    def product_of(w_ref):
        return lax.dot_general(
            back_ref[...],
            weight_tile(w_ref),
            (((1,), (1,)), ((), ())),
            preferred_element_type=jnp.float32,
        )


    def emit(product, offset):
        for g in range(act_ref.shape[1] // shard):
            cols = pl.ds(pl.multiple_of(g * shard + offset, HALF), HALF)
            normed = act_ref[:, cols].astype(jnp.float32) / rms_ref[...]
            part = product[:, g * HALF : (g + 1) * HALF].reshape(groups, tokens, HALF)
            out_ref[g, :, pl.ds(pl.multiple_of(offset, HALF), HALF)] = jnp.sum(
                part * normed[None], axis=1
            )

    core = core_ref[0]
    emit(product_of(w1_ref), core * HALF)
    emit(product_of(w2_ref), (1 - core) * HALF)


def backward_terms(core, back_rows, first, second, activations, rms, groups):
    tokens, width = activations.shape
    keys = first.shape[2]
    tile = 2 * BWD_TILE
    shards = tile // (2 * HALF)
    return pl.pallas_call(
        backward_kernel,
        grid_spec=pltpu.PrefetchScalarGridSpec(
            num_scalar_prefetch=1,
            grid=(width // tile,),
            in_specs=[
                pl.BlockSpec((groups * tokens, keys), lambda k, c: (0, 0)),
                pl.BlockSpec((shards, HALF, keys), lambda k, c: (k, 0, 0)),
                pl.BlockSpec((shards, HALF, keys), lambda k, c: (k, 0, 0)),
                pl.BlockSpec((tokens, tile), lambda k, c: (0, k)),
                pl.BlockSpec((tokens, HALF), lambda k, c: (0, 0)),
            ],
            out_specs=pl.BlockSpec((shards, groups, 2 * HALF), lambda k, c: (k, 0, 0)),
        ),
        out_shape=jax.ShapeDtypeStruct((width // (2 * HALF), groups, 2 * HALF), jnp.float32),
        compiler_params=pltpu.CompilerParams(dimension_semantics=("arbitrary",)),
    )(core, back_rows, first, second, activations, rms)


def per_device(activations, gain, key_weight, key_gain, cotangent, directions):
    tokens_dev = activations.shape[0]
    total_tokens = tokens_dev * lax.axis_size("dp") * lax.axis_size("fsdp")
    values = activations.astype(jnp.float32)
    rms = jnp.sqrt(jnp.mean(values * values, axis=1, keepdims=True) + 1e-05)
    rms = jnp.broadcast_to(rms, (tokens_dev, HALF))
    groups = directions.shape[1] + 1
    core = (lax.axis_index("dp") % 2).astype(jnp.int32).reshape(1)

    first, second = gather_weight(key_weight, gain, directions)
    kg_row = key_gain[None, :]

    back_rows = forward_rows(core, activations, rms, first, second, cotangent, kg_row)
    partial_terms = backward_terms(core, back_rows, first, second, activations, rms, groups)
    shared_rows = jnp.sum(lax.all_to_all(partial_terms, "fsdp", 0, 0, tiled=True), axis=0)
    summed = sum_over_pairs(shared_rows, "dp") / math.sqrt(total_tokens)
    images = summed[1:]
    gram_matrix = of_everyone(
        jnp.dot(images, images.T, precision=lax.Precision.HIGHEST), "fsdp"
    )
    factor = jnp.linalg.cholesky(gram_matrix)
    ortho_basis = math.sqrt(D) * jax.scipy.linalg.solve_triangular(factor, images, lower=True)
    return (ortho_basis.T, summed[0])


def solution(mesh):
    placed = (
        P(("dp", "fsdp"), None),
        P("fsdp"),
        P("fsdp", None),
        P(),
        P(("dp", "fsdp"), None),
        P("fsdp", None),
    )
    return jax.shard_map(
        per_device,
        mesh=mesh,
        in_specs=placed,
        out_specs=(P("fsdp", None), P("fsdp")),
        check_vma=False,
    )
```
